512 devices in a mesh: ka: 64 (over y, z_hi, x), vert: 8 (over z_lo, core).
Axes of the slice: x: 4, y: 8, z: 8 (z_hi: 2, z_lo: 4; z = z_hi * 4 + z_lo), core: 2. Of those that a mesh axis runs over, the one named last changes fastest.
Arguments:
- trial_vector: bfloat16 [64, 112, 896], P('ka'), may hold values from -6 to 6
- left_factor: bfloat16 [64, 2, 256, 12544], P('ka', None, 'vert'), may hold values from -0.03125 to 0.03125
- right_factor: bfloat16 [64, 2, 256, 12544], P(None, None, 'vert', 'ka'), may hold values from -0.5 to 0.5
- kb_table: int32 [64], replicated, may hold values from 0 to 63, as said below
- vir_energy: float32 [64, 112], replicated, may hold values from 0.2 to 1.5
- pair_energy: float32 [8], replicated, may hold values from -2 to -0.5
Outputs:
- sigma_vector: bfloat16 [64, 112, 896], P('ka', 'vert')
The draws below stay inside these ranges and needn't reach their ends.
Inputs may be any that keep to these rules, and one draw needn't show every extreme that they name: kb_table[k] = (S - k) mod 64 for one S per draw, the sum of the window's ki and kj.
All inputs are finite; a program needn't handle non-finite values.
Results may differ from the reference program's by a relative error of at most 0.0027.
Values may be sent and summed in bfloat16 or wider, within the bound.
No kernel may reach another device: no remote copies, remote signals or barrier semaphores. Data moves between devices by JAX's collectives and lax.ppermute only.
A program may use at most 64 MiB of HBM per device.

```python
import jax
import jax.numpy as jnp
from jax import lax

NV = 112
NAUX = 256
PAIRS = 8
TRANSFERS = 2
NK = 64


def draw_kb_table(key, part):
    momentum_sum = jax.random.randint(jax.random.fold_in(key, 11), (), 0, NK, dtype=jnp.int32)
    labels = jnp.arange(NK, dtype=jnp.int32)
    return (momentum_sum - labels) % NK


def shard_levels(rng, shape, shards, smallest, largest):
    def one(axis_at, blocks):
        heights = jax.random.uniform(jax.random.fold_in(jax.random.fold_in(rng, 6), axis_at), (blocks,), jnp.float32, smallest / len(shards), largest / len(shards))
        return jnp.repeat(jnp.exp(heights), shape[axis_at] // blocks).reshape((-1,) + (1,) * (len(shape) - axis_at - 1))

    loudness = one(*shards[0])
    for cut in shards[1:]:
        loudness = loudness * one(*cut)
    return loudness


def scatter_about(own_key, dims, scale, reach, pieces=(), kind=jnp.bfloat16):
    factor_of = shard_levels(own_key, dims, pieces, -0.22, 0.18) if pieces else 1.0
    entries = jax.random.normal(own_key, dims, jnp.float32) * scale * factor_of
    return jnp.minimum(jnp.maximum(entries, -reach), reach).astype(kind)


def setup_inputs(seed: int = 0) -> dict:
    streams_of = jax.random.split(jax.random.key(seed), 7)
    return {
        "trial_vector": scatter_about(streams_of[0], (NK, NV, PAIRS * NV), 1.0, 6.0, ((0, 64),)),
        "left_factor": scatter_about(streams_of[1], (NK, TRANSFERS, NAUX, NV * NV), (NV * NAUX) ** -0.5, 0.03125, ((0, 64), (2, 8))),
        "right_factor": scatter_about(streams_of[2], (NK, TRANSFERS, NAUX, NV * NV), NV ** -0.5, 0.5, ((2, 8), (3, 64))),
        "kb_table": draw_kb_table(jax.random.fold_in(streams_of[6], 71), 0),
        "vir_energy": jnp.clip(jax.random.uniform(streams_of[4], (NK, NV), jnp.float32, 0.2, 1.5), 0.2, 1.5),
        "pair_energy": jnp.clip(jax.random.uniform(streams_of[5], (PAIRS,), jnp.float32, -2.0, -0.5), -2.0, -0.5),
    }


def reference(trial_vector, left_factor, right_factor, kb_table, vir_energy, pair_energy):
    kpoints = trial_vector.shape[0]
    virtuals = vir_energy.shape[1]
    transfers = left_factor.shape[1]
    auxiliary = left_factor.shape[2]
    pair_count = trial_vector.shape[2] // virtuals
    labels = jnp.arange(kpoints, dtype=jnp.int32)

    def per_block(k_index):
        momentum_b = lax.dynamic_index_in_dim(kb_table, k_index, 0, False)
        right_rows = lax.dynamic_index_in_dim(right_factor, momentum_b, 0, False)
        left_rows = lax.dynamic_index_in_dim(left_factor, k_index, 0, False)
        ladder_sum = jnp.zeros((virtuals, pair_count * virtuals), jnp.float32)
        for transfer in range(transfers):
            source_index = ((k_index - transfer) % kpoints).astype(jnp.int32)
            source_block = lax.dynamic_index_in_dim(trial_vector, source_index, 0, False).astype(jnp.float32)
            trial_rows = source_block.reshape(virtuals * pair_count, virtuals)
            right_block = right_rows[transfer].astype(jnp.float32).reshape(auxiliary, virtuals, virtuals)
            half_sum = jnp.einsum("xd,ldb->lxb", trial_rows, right_block).astype(jnp.bfloat16)
            half_sum = lax.optimization_barrier(half_sum).astype(jnp.float32)
            half_sum = half_sum.reshape(auxiliary, virtuals, pair_count * virtuals)
            left_block = left_rows[transfer].astype(jnp.float32).reshape(auxiliary, virtuals, virtuals)
            ladder_sum = ladder_sum + jnp.einsum("lac,lcy->ay", left_block, half_sum)
        own_rows = lax.dynamic_index_in_dim(trial_vector, k_index, 0, False).astype(jnp.float32)
        own_rows = own_rows.reshape(virtuals, pair_count, virtuals)
        energy_a = lax.dynamic_index_in_dim(vir_energy, k_index, 0, False)
        energy_b = lax.dynamic_index_in_dim(vir_energy, momentum_b, 0, False)
        shift_energy = (energy_a[:, None, None] + energy_b[None, None, :]) - pair_energy[None, :, None]
        combined = ladder_sum + (shift_energy * own_rows).reshape(virtuals, pair_count * virtuals)
        return combined.astype(jnp.bfloat16)

    return lax.map(per_block, labels)
```

```python
import functools

import jax
import jax.numpy as jnp
from jax import lax
from jax.experimental import pallas as pl
from jax.experimental.pallas import tpu as pltpu
from jax.sharding import PartitionSpec as P


def shifted(value, axis, steps):
    count = lax.axis_size(axis)
    pairs = [(source, (source + steps) % count) for source in range(count)]
    return lax.ppermute(value, axis, pairs)


def ladder_kernel(ct_ref, tt_ref, b_ref, out_ref, *, chunk, nv, pairs, lanes):
    q = pl.program_id(0)
    j = pl.program_id(1)

    @pl.when((q == 0) & (j == 0))
    def _():
        out_ref[...] = jnp.zeros_like(out_ref)

    half = jnp.dot(ct_ref[0], tt_ref[0], preferred_element_type=jnp.float32)
    half = half.astype(jnp.bfloat16)
    acc = out_ref[...]
    for l in range(chunk):
        rows = half[l * nv:(l + 1) * nv]
        stacked = jnp.concatenate(
            [rows[:, p * lanes:p * lanes + nv] for p in range(pairs)], axis=0
        )
        acc = acc + lax.dot_general(
            stacked, b_ref[0, l], (((1,), (1,)), ((), ())),
            preferred_element_type=jnp.float32,
        )
    out_ref[...] = acc


def ladder_transposed(ct, tt, bq, chunk=8):
    transfers, rows, nv = ct.shape
    aux = bq.shape[1]

    pairs = tt.shape[2] // 128
    lanes = 128
    steps = aux // chunk
    kernel = functools.partial(ladder_kernel, chunk=chunk, nv=nv, pairs=pairs, lanes=lanes)
    flops = 2 * transfers * aux * nv * nv * (pairs * lanes + pairs * nv)
    return pl.pallas_call(
        kernel,
        out_shape=jax.ShapeDtypeStruct((pairs * nv, nv), jnp.float32),
        grid=(transfers, steps),
        in_specs=[
            pl.BlockSpec((1, chunk * nv, nv), lambda q, j: (q, j, 0)),
            pl.BlockSpec((1, nv, pairs * lanes), lambda q, j: (q, 0, 0)),
            pl.BlockSpec((1, chunk, nv, nv), lambda q, j: (q, j, 0, 0)),
        ],
        out_specs=pl.BlockSpec((pairs * nv, nv), lambda q, j: (0, 0)),
        compiler_params=pltpu.CompilerParams(
            dimension_semantics=("arbitrary", "arbitrary"),
            vmem_limit_bytes=48 * 1024 * 1024,
        ),
        cost_estimate=pl.CostEstimate(
            flops=flops, transcendentals=0,
            bytes_accessed=2 * (ct.size + tt.size + bq.size) + 4 * pairs * nv * nv,
        ),
    )(ct, tt, bq)


def trial_transposed(block, virtuals, pair_count):
    t = block.reshape(virtuals, pair_count, virtuals)
    t = jnp.transpose(t, (2, 1, 0))
    t = jnp.pad(t, ((0, 0), (0, 0), (0, 128 - virtuals)))
    return t.reshape(virtuals, pair_count * 128)


def shards(trial_vector, left_factor, right_factor, kb_table, vir_energy, pair_energy):
    kpoints = vir_energy.shape[0]
    virtuals = vir_energy.shape[1]
    transfers = left_factor.shape[1]
    aux_local = left_factor.shape[2]
    pair_count = trial_vector.shape[2] // virtuals
    ordered = right_factor.at[kb_table].get(mode="promise_in_bounds")
    arrived = lax.all_to_all(ordered, "ka", split_axis=0, concat_axis=3, tiled=True)[0]
    right = arrived.reshape(transfers, aux_local, virtuals, virtuals)
    ct = jnp.swapaxes(right, 2, 3).reshape(transfers, aux_local * virtuals, virtuals)
    own_block = trial_vector[0]
    blocks = [own_block] + [
        shifted(trial_vector, "ka", t)[0] for t in range(1, transfers)
    ]
    tt = jnp.stack([trial_transposed(b, virtuals, pair_count) for b in blocks])
    bq = left_factor[0].reshape(transfers, aux_local, virtuals, virtuals)
    ladder_t = ladder_transposed(ct, tt, bq)
    ladder_sum = ladder_t.T
    ladder = lax.psum_scatter(ladder_sum, "vert", scatter_dimension=0, tiled=True)
    slab_width = ladder.shape[0]
    offset = lax.axis_index("vert") * slab_width
    labels = jnp.arange(kpoints, dtype=jnp.int32)
    owner_index = lax.axis_index("ka")
    momentum_b = jnp.sum(jnp.where(labels == owner_index, kb_table, 0))
    energy_rows = jnp.sum(jnp.where((labels == owner_index)[:, None], vir_energy, 0.0), axis=0)
    energy_other = jnp.sum(jnp.where((labels == momentum_b)[:, None], vir_energy, 0.0), axis=0)
    energy_a = lax.dynamic_slice_in_dim(energy_rows, offset, slab_width, 0)
    own_rows = lax.dynamic_slice_in_dim(own_block, offset, slab_width, 0).astype(jnp.float32)
    own_rows = own_rows.reshape(slab_width, pair_count, virtuals)
    shift_energy = (
        energy_a[:, None, None] + energy_other[None, None, :] - pair_energy[None, :, None]
    )
    combined = ladder + (shift_energy * own_rows).reshape(slab_width, pair_count * virtuals)
    return combined.astype(jnp.bfloat16)[None]


def solution(mesh):
    in_specs = (
        P("ka", None, None),
        P("ka", None, "vert", None),
        P(None, None, "vert", "ka"),
        P(),
        P(),
        P(),
    )
    out_specs = P("ka", "vert", None)
    return jax.shard_map(shards, mesh=mesh, in_specs=in_specs, out_specs=out_specs, check_vma=False)
```

```python
import functools

import jax
import jax.numpy as jnp
from jax import lax
from jax.experimental import pallas as pl
from jax.experimental.pallas import tpu as pltpu
from jax.sharding import PartitionSpec as P


def shifted(value, axis, steps):
    count = lax.axis_size(axis)
    pairs = [(source, (source + steps) % count) for source in range(count)]
    return lax.ppermute(value, axis, pairs)


def ladder_kernel(ct_ref, tt_ref, b_ref, acc_ref, out_ref, *, chunk, nv, pairs, lanes):
    j = pl.program_id(0)

    @pl.when(j == 0)
    def _():
        out_ref[...] = acc_ref[...]

    half = jnp.dot(ct_ref[...], tt_ref[...], preferred_element_type=jnp.float32)
    half = half.astype(jnp.bfloat16)
    acc = out_ref[...]
    for l in range(chunk):
        rows = half[l * nv:(l + 1) * nv]
        stacked = jnp.concatenate(
            [rows[:, p * lanes:p * lanes + nv] for p in range(pairs)], axis=0
        )
        acc = acc + lax.dot_general(
            stacked, b_ref[l], (((1,), (1,)), ((), ())),
            preferred_element_type=jnp.float32,
        )
    out_ref[...] = acc


def ladder_transposed(ct, tt, bq, acc, chunk=8):
    rows, nv = ct.shape
    aux = bq.shape[0]
    lanes = 128
    pairs = tt.shape[1] // lanes
    steps = aux // chunk
    kernel = functools.partial(ladder_kernel, chunk=chunk, nv=nv, pairs=pairs, lanes=lanes)
    flops = 2 * aux * nv * nv * (pairs * lanes + pairs * nv)
    return pl.pallas_call(
        kernel,
        out_shape=jax.ShapeDtypeStruct((pairs * nv, nv), jnp.float32),
        grid=(steps,),
        in_specs=[
            pl.BlockSpec((chunk * nv, nv), lambda j: (j, 0)),
            pl.BlockSpec((nv, pairs * lanes), lambda j: (0, 0)),
            pl.BlockSpec((chunk, nv, nv), lambda j: (j, 0, 0)),
            pl.BlockSpec((pairs * nv, nv), lambda j: (0, 0)),
        ],
        out_specs=pl.BlockSpec((pairs * nv, nv), lambda j: (0, 0)),
        input_output_aliases={3: 0},
        compiler_params=pltpu.CompilerParams(
            dimension_semantics=("arbitrary",),
            vmem_limit_bytes=48 * 1024 * 1024,
        ),
        cost_estimate=pl.CostEstimate(
            flops=flops, transcendentals=0,
            bytes_accessed=2 * (ct.size + tt.size + bq.size) + 8 * pairs * nv * nv,
        ),
    )(ct, tt, bq, acc)


def trial_transposed(block, virtuals, pair_count):
    t = block.reshape(virtuals, pair_count, virtuals)
    t = jnp.transpose(t, (2, 1, 0))
    t = jnp.pad(t, ((0, 0), (0, 0), (0, 128 - virtuals)))
    return t.reshape(virtuals, pair_count * 128)


def shards(trial_vector, left_factor, right_factor, kb_table, vir_energy, pair_energy):
    kpoints = vir_energy.shape[0]
    virtuals = vir_energy.shape[1]
    transfers = left_factor.shape[1]
    aux_local = left_factor.shape[2]
    pair_count = trial_vector.shape[2] // virtuals
    ordered = right_factor.at[kb_table].get(mode="promise_in_bounds")
    own_block = trial_vector[0]
    bq = left_factor[0].reshape(transfers, aux_local, virtuals, virtuals)
    ladder_t = jnp.zeros((pair_count * virtuals, virtuals), jnp.float32)
    previous = None
    for transfer in range(transfers):
        piece = ordered[:, transfer]
        if previous is not None:
            piece, previous = lax.optimization_barrier((piece, previous))
        arrived = lax.all_to_all(piece, "ka", split_axis=0, concat_axis=2, tiled=True)[0]
        previous = arrived
        right = arrived.reshape(aux_local, virtuals, virtuals)
        ct = jnp.swapaxes(right, 1, 2).reshape(aux_local * virtuals, virtuals)
        block = own_block if transfer == 0 else shifted(trial_vector, "ka", transfer)[0]
        tt = trial_transposed(block, virtuals, pair_count)
        ladder_t = ladder_transposed(ct, tt, bq[transfer], ladder_t)
    ladder_sum = ladder_t.T
    vert = lax.axis_size("vert")
    slab_width = virtuals // vert
    ladder = lax.all_to_all(
        ladder_sum.reshape(vert, slab_width, -1), "vert", 0, 0, tiled=True
    ).sum(0)
    offset = lax.axis_index("vert") * slab_width
    labels = jnp.arange(kpoints, dtype=jnp.int32)
    owner_index = lax.axis_index("ka")
    momentum_b = jnp.sum(jnp.where(labels == owner_index, kb_table, 0))
    energy_rows = jnp.sum(jnp.where((labels == owner_index)[:, None], vir_energy, 0.0), axis=0)
    energy_other = jnp.sum(jnp.where((labels == momentum_b)[:, None], vir_energy, 0.0), axis=0)
    energy_a = lax.dynamic_slice_in_dim(energy_rows, offset, slab_width, 0)
    own_rows = lax.dynamic_slice_in_dim(own_block, offset, slab_width, 0).astype(jnp.float32)
    own_rows = own_rows.reshape(slab_width, pair_count, virtuals)
    shift_energy = (
        energy_a[:, None, None] + energy_other[None, None, :] - pair_energy[None, :, None]
    )
    combined = ladder + (shift_energy * own_rows).reshape(slab_width, pair_count * virtuals)
    return combined.astype(jnp.bfloat16)[None]


def solution(mesh):
    in_specs = (
        P("ka", None, None),
        P("ka", None, "vert", None),
        P(None, None, "vert", "ka"),
        P(),
        P(),
        P(),
    )
    out_specs = P("ka", "vert", None)
    return jax.shard_map(shards, mesh=mesh, in_specs=in_specs, out_specs=out_specs, check_vma=False)
```

```python
import functools

import jax
import jax.numpy as jnp
from jax import lax
from jax.experimental import pallas as pl
from jax.experimental.pallas import tpu as pltpu
from jax.sharding import PartitionSpec as P


def shifted(value, axis, steps):
    count = lax.axis_size(axis)
    pairs = [(source, (source + steps) % count) for source in range(count)]
    return lax.ppermute(value, axis, pairs)


def ladder_kernel(ct_ref, tt_ref, b_ref, acc_ref, out_ref, *, chunk, nv, pairs, lanes):
    j = pl.program_id(0)

    @pl.when(j == 0)
    def _():
        out_ref[...] = acc_ref[...]

    half = jnp.dot(ct_ref[...], tt_ref[...], preferred_element_type=jnp.float32)
    half = half.astype(jnp.bfloat16)
    acc = out_ref[...]
    for l in range(chunk):
        rows = half[l * nv:(l + 1) * nv]
        stacked = jnp.concatenate(
            [rows[:, p * lanes:p * lanes + nv] for p in range(pairs)], axis=0
        )
        acc = acc + lax.dot_general(
            stacked, b_ref[l], (((1,), (1,)), ((), ())),
            preferred_element_type=jnp.float32,
        )
    out_ref[...] = acc


def ladder_transposed(ct, tt, bq, acc, chunk=8):
    rows, nv = ct.shape
    aux = bq.shape[0]
    lanes = 128
    pairs = tt.shape[1] // lanes
    steps = aux // chunk
    kernel = functools.partial(ladder_kernel, chunk=chunk, nv=nv, pairs=pairs, lanes=lanes)
    flops = 2 * aux * nv * nv * (pairs * lanes + pairs * nv)
    return pl.pallas_call(
        kernel,
        out_shape=jax.ShapeDtypeStruct((pairs * nv, nv), jnp.float32),
        grid=(steps,),
        in_specs=[
            pl.BlockSpec((chunk * nv, nv), lambda j: (j, 0)),
            pl.BlockSpec((nv, pairs * lanes), lambda j: (0, 0)),
            pl.BlockSpec((chunk, nv, nv), lambda j: (j, 0, 0)),
            pl.BlockSpec((pairs * nv, nv), lambda j: (0, 0)),
        ],
        out_specs=pl.BlockSpec((pairs * nv, nv), lambda j: (0, 0)),
        input_output_aliases={3: 0},
        compiler_params=pltpu.CompilerParams(
            dimension_semantics=("arbitrary",),
            vmem_limit_bytes=48 * 1024 * 1024,
        ),
        cost_estimate=pl.CostEstimate(
            flops=flops, transcendentals=0,
            bytes_accessed=2 * (ct.size + tt.size + bq.size) + 8 * pairs * nv * nv,
        ),
    )(ct, tt, bq, acc)


def trial_transposed(block, virtuals, pair_count):
    t = block.reshape(virtuals, pair_count, virtuals)
    t = jnp.transpose(t, (2, 1, 0))
    t = jnp.pad(t, ((0, 0), (0, 0), (0, 128 - virtuals)))
    return t.reshape(virtuals, pair_count * 128)


def shards(trial_vector, left_factor, right_factor, kb_table, vir_energy, pair_energy):
    kpoints = vir_energy.shape[0]
    virtuals = vir_energy.shape[1]
    transfers = left_factor.shape[1]
    aux_local = left_factor.shape[2]
    pair_count = trial_vector.shape[2] // virtuals
    ordered = right_factor.at[kb_table].get(mode="promise_in_bounds")
    flat = ordered.size // kpoints
    send = ordered.reshape(kpoints, flat // 128, 128)
    received = lax.all_to_all(send, "ka", split_axis=0, concat_axis=0, tiled=True)
    arrived = received.reshape(kpoints, transfers, aux_local, -1)
    arrived = jnp.transpose(arrived, (1, 2, 0, 3)).reshape(transfers, aux_local, virtuals, virtuals)
    ct_all = jnp.swapaxes(arrived, 2, 3).reshape(transfers, aux_local * virtuals, virtuals)
    own_block = trial_vector[0]
    bq = left_factor[0].reshape(transfers, aux_local, virtuals, virtuals)
    ladder_t = jnp.zeros((pair_count * virtuals, virtuals), jnp.float32)
    for transfer in range(transfers):
        block = own_block if transfer == 0 else shifted(trial_vector, "ka", transfer)[0]
        tt = trial_transposed(block, virtuals, pair_count)
        ladder_t = ladder_transposed(ct_all[transfer], tt, bq[transfer], ladder_t)
    ladder_sum = ladder_t.T
    vert = lax.axis_size("vert")
    slab_width = virtuals // vert
    ladder = lax.psum_scatter(
        ladder_sum.reshape(vert, slab_width, -1), "vert", scatter_dimension=0, tiled=True
    )[0]
    offset = lax.axis_index("vert") * slab_width
    labels = jnp.arange(kpoints, dtype=jnp.int32)
    owner_index = lax.axis_index("ka")
    momentum_b = jnp.sum(jnp.where(labels == owner_index, kb_table, 0))
    energy_rows = jnp.sum(jnp.where((labels == owner_index)[:, None], vir_energy, 0.0), axis=0)
    energy_other = jnp.sum(jnp.where((labels == momentum_b)[:, None], vir_energy, 0.0), axis=0)
    energy_a = lax.dynamic_slice_in_dim(energy_rows, offset, slab_width, 0)
    own_rows = lax.dynamic_slice_in_dim(own_block, offset, slab_width, 0).astype(jnp.float32)
    own_rows = own_rows.reshape(slab_width, pair_count, virtuals)
    shift_energy = (
        energy_a[:, None, None] + energy_other[None, None, :] - pair_energy[None, :, None]
    )
    combined = ladder + (shift_energy * own_rows).reshape(slab_width, pair_count * virtuals)
    return combined.astype(jnp.bfloat16)[None]


def solution(mesh):
    in_specs = (
        P("ka", None, None),
        P("ka", None, "vert", None),
        P(None, None, "vert", "ka"),
        P(),
        P(),
        P(),
    )
    out_specs = P("ka", "vert", None)
    return jax.shard_map(shards, mesh=mesh, in_specs=in_specs, out_specs=out_specs, check_vma=False)
```

```python
import functools

import jax
import jax.numpy as jnp
from jax import lax
from jax.experimental import pallas as pl
from jax.experimental.pallas import tpu as pltpu
from jax.sharding import PartitionSpec as P


def shifted(value, axis, steps):
    count = lax.axis_size(axis)
    pairs = [(source, (source + steps) % count) for source in range(count)]
    return lax.ppermute(value, axis, pairs)


def ladder_kernel(ct_ref, tt_ref, b_ref, acc_ref, out_ref, *, chunk, nv, pairs, lanes):
    j = pl.program_id(0)

    @pl.when(j == 0)
    def _():
        out_ref[...] = acc_ref[...]

    half = jnp.dot(ct_ref[...], tt_ref[...], preferred_element_type=jnp.float32)
    half = half.astype(jnp.bfloat16)
    acc = out_ref[...]
    for l in range(chunk):
        rows = half[l * nv:(l + 1) * nv]
        stacked = jnp.concatenate(
            [rows[:, p * lanes:p * lanes + nv] for p in range(pairs)], axis=0
        )
        acc = acc + lax.dot_general(
            stacked, b_ref[l], (((1,), (1,)), ((), ())),
            preferred_element_type=jnp.float32,
        )
    out_ref[...] = acc


def ladder_transposed(ct, tt, bq, acc, chunk=8):
    rows, nv = ct.shape
    aux = bq.shape[0]
    lanes = 128
    pairs = tt.shape[1] // lanes
    steps = aux // chunk
    kernel = functools.partial(ladder_kernel, chunk=chunk, nv=nv, pairs=pairs, lanes=lanes)
    flops = 2 * aux * nv * nv * (pairs * lanes + pairs * nv)
    return pl.pallas_call(
        kernel,
        out_shape=jax.ShapeDtypeStruct((pairs * nv, nv), jnp.float32),
        grid=(steps,),
        in_specs=[
            pl.BlockSpec((chunk * nv, nv), lambda j: (j, 0)),
            pl.BlockSpec((nv, pairs * lanes), lambda j: (0, 0)),
            pl.BlockSpec((chunk, nv, nv), lambda j: (j, 0, 0)),
            pl.BlockSpec((pairs * nv, nv), lambda j: (0, 0)),
        ],
        out_specs=pl.BlockSpec((pairs * nv, nv), lambda j: (0, 0)),
        input_output_aliases={3: 0},
        compiler_params=pltpu.CompilerParams(
            dimension_semantics=("arbitrary",),
            vmem_limit_bytes=48 * 1024 * 1024,
        ),
        cost_estimate=pl.CostEstimate(
            flops=flops, transcendentals=0,
            bytes_accessed=2 * (ct.size + tt.size + bq.size) + 8 * pairs * nv * nv,
        ),
    )(ct, tt, bq, acc)


def trial_transposed(block, virtuals, pair_count):
    t = block.reshape(virtuals, pair_count, virtuals)
    t = jnp.transpose(t, (2, 1, 0))
    t = jnp.pad(t, ((0, 0), (0, 0), (0, 128 - virtuals)))
    return t.reshape(virtuals, pair_count * 128)


def shards(trial_vector, left_factor, right_factor, kb_table, vir_energy, pair_energy):
    kpoints = vir_energy.shape[0]
    virtuals = vir_energy.shape[1]
    transfers = left_factor.shape[1]
    aux_local = left_factor.shape[2]
    pair_count = trial_vector.shape[2] // virtuals
    own_block = trial_vector[0]
    bq = left_factor[0].reshape(transfers, aux_local, virtuals, virtuals)
    arrivals = []
    for transfer in range(transfers):
        piece = right_factor[:, transfer].at[kb_table].get(mode="promise_in_bounds")
        if arrivals:
            piece, arrivals[-1], bq = lax.optimization_barrier((piece, arrivals[-1], bq))
        arrivals.append(
            lax.all_to_all(piece, "ka", split_axis=0, concat_axis=2, tiled=True)[0]
        )
    ladder_t = jnp.zeros((pair_count * virtuals, virtuals), jnp.float32)
    for transfer in range(transfers):
        right = arrivals[transfer].reshape(aux_local, virtuals, virtuals)
        ct = jnp.swapaxes(right, 1, 2).reshape(aux_local * virtuals, virtuals)
        block = own_block if transfer == 0 else shifted(trial_vector, "ka", transfer)[0]
        tt = trial_transposed(block, virtuals, pair_count)
        ladder_t = ladder_transposed(ct, tt, bq[transfer], ladder_t)
    ladder_sum = ladder_t.T
    vert = lax.axis_size("vert")
    slab_width = virtuals // vert
    ladder = lax.all_to_all(
        ladder_sum.reshape(vert, slab_width, -1), "vert", 0, 0, tiled=True
    ).sum(0)
    offset = lax.axis_index("vert") * slab_width
    labels = jnp.arange(kpoints, dtype=jnp.int32)
    owner_index = lax.axis_index("ka")
    momentum_b = jnp.sum(jnp.where(labels == owner_index, kb_table, 0))
    energy_rows = jnp.sum(jnp.where((labels == owner_index)[:, None], vir_energy, 0.0), axis=0)
    energy_other = jnp.sum(jnp.where((labels == momentum_b)[:, None], vir_energy, 0.0), axis=0)
    energy_a = lax.dynamic_slice_in_dim(energy_rows, offset, slab_width, 0)
    own_rows = lax.dynamic_slice_in_dim(own_block, offset, slab_width, 0).astype(jnp.float32)
    own_rows = own_rows.reshape(slab_width, pair_count, virtuals)
    shift_energy = (
        energy_a[:, None, None] + energy_other[None, None, :] - pair_energy[None, :, None]
    )
    combined = ladder + (shift_energy * own_rows).reshape(slab_width, pair_count * virtuals)
    return combined.astype(jnp.bfloat16)[None]


def solution(mesh):
    in_specs = (
        P("ka", None, None),
        P("ka", None, "vert", None),
        P(None, None, "vert", "ka"),
        P(),
        P(),
        P(),
    )
    out_specs = P("ka", "vert", None)
    return jax.shard_map(shards, mesh=mesh, in_specs=in_specs, out_specs=out_specs, check_vma=False)
```

```python
import functools

import jax
import jax.numpy as jnp
from jax import lax
from jax.experimental import pallas as pl
from jax.experimental.pallas import tpu as pltpu
from jax.sharding import PartitionSpec as P


def shifted(value, axis, steps):
    count = lax.axis_size(axis)
    pairs = [(source, (source + steps) % count) for source in range(count)]
    return lax.ppermute(value, axis, pairs)


def ladder_kernel(ct_ref, tt_ref, b_ref, acc_ref, out_ref, *, chunk, nv, pairs, lanes):
    j = pl.program_id(0)

    @pl.when(j == 0)
    def _():
        out_ref[...] = acc_ref[...]

    half = jnp.dot(ct_ref[...], tt_ref[...], preferred_element_type=jnp.float32)
    half = half.astype(jnp.bfloat16)
    acc = out_ref[...]
    for l in range(chunk):
        rows = half[l * nv:(l + 1) * nv]
        stacked = jnp.concatenate(
            [rows[:, p * lanes:p * lanes + nv] for p in range(pairs)], axis=0
        )
        acc = acc + lax.dot_general(
            stacked, b_ref[l], (((1,), (1,)), ((), ())),
            preferred_element_type=jnp.float32,
        )
    out_ref[...] = acc


def ladder_transposed(ct, tt, bq, acc, chunk=8):
    rows, nv = ct.shape
    aux = bq.shape[0]
    lanes = 128
    pairs = tt.shape[1] // lanes
    steps = aux // chunk
    kernel = functools.partial(ladder_kernel, chunk=chunk, nv=nv, pairs=pairs, lanes=lanes)
    flops = 2 * aux * nv * nv * (pairs * lanes + pairs * nv)
    return pl.pallas_call(
        kernel,
        out_shape=jax.ShapeDtypeStruct((pairs * nv, nv), jnp.float32),
        grid=(steps,),
        in_specs=[
            pl.BlockSpec((chunk * nv, nv), lambda j: (j, 0)),
            pl.BlockSpec((nv, pairs * lanes), lambda j: (0, 0)),
            pl.BlockSpec((chunk, nv, nv), lambda j: (j, 0, 0)),
            pl.BlockSpec((pairs * nv, nv), lambda j: (0, 0)),
        ],
        out_specs=pl.BlockSpec((pairs * nv, nv), lambda j: (0, 0)),
        input_output_aliases={3: 0},
        compiler_params=pltpu.CompilerParams(
            dimension_semantics=("arbitrary",),
            vmem_limit_bytes=48 * 1024 * 1024,
        ),
        cost_estimate=pl.CostEstimate(
            flops=flops, transcendentals=0,
            bytes_accessed=2 * (ct.size + tt.size + bq.size) + 8 * pairs * nv * nv,
        ),
    )(ct, tt, bq, acc)


def trial_transposed(block, virtuals, pair_count):
    t = block.reshape(virtuals, pair_count, virtuals)
    t = jnp.transpose(t, (2, 1, 0))
    t = jnp.pad(t, ((0, 0), (0, 0), (0, 128 - virtuals)))
    return t.reshape(virtuals, pair_count * 128)


def shards(trial_vector, left_factor, right_factor, kb_table, vir_energy, pair_energy):
    kpoints = vir_energy.shape[0]
    virtuals = vir_energy.shape[1]
    transfers = left_factor.shape[1]
    aux_local = left_factor.shape[2]
    pair_count = trial_vector.shape[2] // virtuals
    own_block = trial_vector[0]
    bq = left_factor[0].reshape(transfers, aux_local, virtuals, virtuals)
    blocks = [own_block] + [
        shifted(trial_vector, "ka", transfer)[0] for transfer in range(1, transfers)
    ]
    arrivals = []
    for transfer in range(transfers):
        piece = right_factor[:, transfer].at[kb_table].get(mode="promise_in_bounds")
        if arrivals:
            piece, arrivals[-1], bq, blocks = lax.optimization_barrier(
                (piece, arrivals[-1], bq, blocks)
            )
        arrivals.append(
            lax.all_to_all(piece, "ka", split_axis=0, concat_axis=2, tiled=True)[0]
        )
    ladder_t = jnp.zeros((pair_count * virtuals, virtuals), jnp.float32)
    for transfer in range(transfers):
        right = arrivals[transfer].reshape(aux_local, virtuals, virtuals)
        ct = jnp.swapaxes(right, 1, 2).reshape(aux_local * virtuals, virtuals)
        tt = trial_transposed(blocks[transfer], virtuals, pair_count)
        ladder_t = ladder_transposed(ct, tt, bq[transfer], ladder_t)
    ladder_sum = ladder_t.T
    vert = lax.axis_size("vert")
    slab_width = virtuals // vert
    ladder = lax.all_to_all(
        ladder_sum.reshape(vert, slab_width, -1), "vert", 0, 0, tiled=True
    ).sum(0)
    offset = lax.axis_index("vert") * slab_width
    labels = jnp.arange(kpoints, dtype=jnp.int32)
    owner_index = lax.axis_index("ka")
    momentum_b = jnp.sum(jnp.where(labels == owner_index, kb_table, 0))
    energy_rows = jnp.sum(jnp.where((labels == owner_index)[:, None], vir_energy, 0.0), axis=0)
    energy_other = jnp.sum(jnp.where((labels == momentum_b)[:, None], vir_energy, 0.0), axis=0)
    energy_a = lax.dynamic_slice_in_dim(energy_rows, offset, slab_width, 0)
    own_rows = lax.dynamic_slice_in_dim(blocks[0], offset, slab_width, 0).astype(jnp.float32)
    own_rows = own_rows.reshape(slab_width, pair_count, virtuals)
    shift_energy = (
        energy_a[:, None, None] + energy_other[None, None, :] - pair_energy[None, :, None]
    )
    combined = ladder + (shift_energy * own_rows).reshape(slab_width, pair_count * virtuals)
    return combined.astype(jnp.bfloat16)[None]


def solution(mesh):
    in_specs = (
        P("ka", None, None),
        P("ka", None, "vert", None),
        P(None, None, "vert", "ka"),
        P(),
        P(),
        P(),
    )
    out_specs = P("ka", "vert", None)
    return jax.shard_map(shards, mesh=mesh, in_specs=in_specs, out_specs=out_specs, check_vma=False)
```

```python
import functools

import jax
import jax.numpy as jnp
from jax import lax
from jax.experimental import pallas as pl
from jax.experimental.pallas import tpu as pltpu
from jax.sharding import PartitionSpec as P


def shifted(value, axis, steps):
    count = lax.axis_size(axis)
    pairs = [(source, (source + steps) % count) for source in range(count)]
    return lax.ppermute(value, axis, pairs)


def ladder_kernel(ct_ref, tt_ref, b_ref, acc_ref, out_ref, *, chunk, nv, pairs, lanes):
    j = pl.program_id(0)

    @pl.when(j == 0)
    def _():
        out_ref[...] = acc_ref[...]

    half = jnp.dot(ct_ref[...], tt_ref[...], preferred_element_type=jnp.float32)
    half = half.astype(jnp.bfloat16)
    acc = out_ref[...]
    for l in range(chunk):
        rows = half[l * nv:(l + 1) * nv]
        stacked = jnp.concatenate(
            [rows[:, p * lanes:p * lanes + nv] for p in range(pairs)], axis=0
        )
        acc = acc + lax.dot_general(
            stacked, b_ref[l], (((1,), (1,)), ((), ())),
            preferred_element_type=jnp.float32,
        )
    out_ref[...] = acc


def ladder_transposed(ct, tt, bq, acc, chunk=8):
    rows, nv = ct.shape
    aux = bq.shape[0]
    lanes = 128
    pairs = tt.shape[1] // lanes
    steps = aux // chunk
    kernel = functools.partial(ladder_kernel, chunk=chunk, nv=nv, pairs=pairs, lanes=lanes)
    flops = 2 * aux * nv * nv * (pairs * lanes + pairs * nv)
    return pl.pallas_call(
        kernel,
        out_shape=jax.ShapeDtypeStruct((pairs * nv, nv), jnp.float32),
        grid=(steps,),
        in_specs=[
            pl.BlockSpec((chunk * nv, nv), lambda j: (j, 0)),
            pl.BlockSpec((nv, pairs * lanes), lambda j: (0, 0)),
            pl.BlockSpec((chunk, nv, nv), lambda j: (j, 0, 0)),
            pl.BlockSpec((pairs * nv, nv), lambda j: (0, 0)),
        ],
        out_specs=pl.BlockSpec((pairs * nv, nv), lambda j: (0, 0)),
        input_output_aliases={3: 0},
        compiler_params=pltpu.CompilerParams(
            dimension_semantics=("arbitrary",),
            vmem_limit_bytes=48 * 1024 * 1024,
        ),
        cost_estimate=pl.CostEstimate(
            flops=flops, transcendentals=0,
            bytes_accessed=2 * (ct.size + tt.size + bq.size) + 8 * pairs * nv * nv,
        ),
    )(ct, tt, bq, acc)


def trial_transposed(block, virtuals, pair_count):
    t = block.reshape(virtuals, pair_count, virtuals)
    t = jnp.transpose(t, (2, 1, 0))
    t = jnp.pad(t, ((0, 0), (0, 0), (0, 128 - virtuals)))
    return t.reshape(virtuals, pair_count * 128)


def shards(trial_vector, left_factor, right_factor, kb_table, vir_energy, pair_energy):
    kpoints = vir_energy.shape[0]
    virtuals = vir_energy.shape[1]
    transfers = left_factor.shape[1]
    aux_local = left_factor.shape[2]
    pair_count = trial_vector.shape[2] // virtuals
    own_block = trial_vector[0]
    bq = left_factor[0].reshape(transfers, aux_local, virtuals, virtuals)
    arrivals = []
    for transfer in range(transfers):
        piece = right_factor[:, transfer].at[kb_table].get(mode="promise_in_bounds")
        if arrivals:
            piece, arrivals[-1], bq = lax.optimization_barrier((piece, arrivals[-1], bq))
        arrivals.append(
            lax.all_to_all(piece, "ka", split_axis=0, concat_axis=2, tiled=True)[0]
        )
    ladder_t = jnp.zeros((pair_count * virtuals, virtuals), jnp.float32)
    trial_now = trial_vector
    for transfer in range(transfers):
        right = arrivals[transfer].reshape(aux_local, virtuals, virtuals)
        ct = jnp.swapaxes(right, 1, 2).reshape(aux_local * virtuals, virtuals)
        if transfer == 0:
            block = own_block
        else:
            trial_now, ladder_t = lax.optimization_barrier((trial_now, ladder_t))
            block = shifted(trial_now, "ka", transfer)[0]
        tt = trial_transposed(block, virtuals, pair_count)
        ladder_t = ladder_transposed(ct, tt, bq[transfer], ladder_t)
    ladder_sum = ladder_t.T
    vert = lax.axis_size("vert")
    slab_width = virtuals // vert
    ladder = lax.all_to_all(
        ladder_sum.reshape(vert, slab_width, -1), "vert", 0, 0, tiled=True
    ).sum(0)
    offset = lax.axis_index("vert") * slab_width
    labels = jnp.arange(kpoints, dtype=jnp.int32)
    owner_index = lax.axis_index("ka")
    momentum_b = jnp.sum(jnp.where(labels == owner_index, kb_table, 0))
    energy_rows = jnp.sum(jnp.where((labels == owner_index)[:, None], vir_energy, 0.0), axis=0)
    energy_other = jnp.sum(jnp.where((labels == momentum_b)[:, None], vir_energy, 0.0), axis=0)
    energy_a = lax.dynamic_slice_in_dim(energy_rows, offset, slab_width, 0)
    own_rows = lax.dynamic_slice_in_dim(own_block, offset, slab_width, 0).astype(jnp.float32)
    own_rows = own_rows.reshape(slab_width, pair_count, virtuals)
    shift_energy = (
        energy_a[:, None, None] + energy_other[None, None, :] - pair_energy[None, :, None]
    )
    combined = ladder + (shift_energy * own_rows).reshape(slab_width, pair_count * virtuals)
    return combined.astype(jnp.bfloat16)[None]


def solution(mesh):
    in_specs = (
        P("ka", None, None),
        P("ka", None, "vert", None),
        P(None, None, "vert", "ka"),
        P(),
        P(),
        P(),
    )
    out_specs = P("ka", "vert", None)
    return jax.shard_map(shards, mesh=mesh, in_specs=in_specs, out_specs=out_specs, check_vma=False)
```

```python
import functools

import jax
import jax.numpy as jnp
from jax import lax
from jax.experimental import pallas as pl
from jax.experimental.pallas import tpu as pltpu
from jax.sharding import PartitionSpec as P


def shifted(value, axis, steps):
    count = lax.axis_size(axis)
    pairs = [(source, (source + steps) % count) for source in range(count)]
    return lax.ppermute(value, axis, pairs)


def ladder_kernel(ct_ref, tt_ref, b_ref, acc_ref, out_ref, *, chunk, nv, pairs, lanes):
    j = pl.program_id(0)

    @pl.when(j == 0)
    def _():
        out_ref[...] = acc_ref[...]

    half = jnp.dot(ct_ref[...], tt_ref[...], preferred_element_type=jnp.float32)
    half = half.astype(jnp.bfloat16)
    acc = out_ref[...]
    for l in range(chunk):
        rows = half[l * nv:(l + 1) * nv]
        stacked = jnp.concatenate(
            [rows[:, p * lanes:p * lanes + nv] for p in range(pairs)], axis=0
        )
        acc = acc + lax.dot_general(
            stacked, b_ref[l], (((1,), (1,)), ((), ())),
            preferred_element_type=jnp.float32,
        )
    out_ref[...] = acc


def ladder_transposed(ct, tt, bq, acc, chunk=8):
    rows, nv = ct.shape
    aux = bq.shape[0]
    lanes = 128
    pairs = tt.shape[1] // lanes
    steps = aux // chunk
    kernel = functools.partial(ladder_kernel, chunk=chunk, nv=nv, pairs=pairs, lanes=lanes)
    flops = 2 * aux * nv * nv * (pairs * lanes + pairs * nv)
    return pl.pallas_call(
        kernel,
        out_shape=jax.ShapeDtypeStruct((pairs * nv, nv), jnp.float32),
        grid=(steps,),
        in_specs=[
            pl.BlockSpec((chunk * nv, nv), lambda j: (j, 0)),
            pl.BlockSpec((nv, pairs * lanes), lambda j: (0, 0)),
            pl.BlockSpec((chunk, nv, nv), lambda j: (j, 0, 0)),
            pl.BlockSpec((pairs * nv, nv), lambda j: (0, 0)),
        ],
        out_specs=pl.BlockSpec((pairs * nv, nv), lambda j: (0, 0)),
        input_output_aliases={3: 0},
        compiler_params=pltpu.CompilerParams(
            dimension_semantics=("arbitrary",),
            vmem_limit_bytes=48 * 1024 * 1024,
        ),
        cost_estimate=pl.CostEstimate(
            flops=flops, transcendentals=0,
            bytes_accessed=2 * (ct.size + tt.size + bq.size) + 8 * pairs * nv * nv,
        ),
    )(ct, tt, bq, acc)


def trial_transposed(block, virtuals, pair_count):
    t = block.reshape(virtuals, pair_count, virtuals)
    t = jnp.transpose(t, (2, 1, 0))
    t = jnp.pad(t, ((0, 0), (0, 0), (0, 128 - virtuals)))
    return t.reshape(virtuals, pair_count * 128)


def shards(trial_vector, left_factor, right_factor, kb_table, vir_energy, pair_energy):
    kpoints = vir_energy.shape[0]
    virtuals = vir_energy.shape[1]
    transfers = left_factor.shape[1]
    aux_local = left_factor.shape[2]
    pair_count = trial_vector.shape[2] // virtuals
    own_block = trial_vector[0]
    bq = left_factor[0].reshape(transfers, aux_local, virtuals, virtuals)
    blocks = [own_block] + [
        shifted(trial_vector, "ka", transfer)[0] for transfer in range(1, transfers)
    ]
    tail = aux_local // 2
    last = transfers - 1
    groups = [
        [(t, 0, aux_local) for t in range(last)] + [(last, 0, aux_local - tail)],
        [(last, aux_local - tail, tail)],
    ]
    arrivals = []
    for group in groups:
        piece = jnp.concatenate(
            [right_factor[:, t, start:start + count] for t, start, count in group], axis=1
        )
        piece = piece.at[kb_table].get(mode="promise_in_bounds")
        if arrivals:
            piece, arrivals[-1], bq, blocks = lax.optimization_barrier(
                (piece, arrivals[-1], bq, blocks)
            )
        arrivals.append(
            lax.all_to_all(piece, "ka", split_axis=0, concat_axis=2, tiled=True)[0]
        )
    ladder_t = jnp.zeros((pair_count * virtuals, virtuals), jnp.float32)
    tts = [trial_transposed(b, virtuals, pair_count) for b in blocks]
    for group, arrived in zip(groups, arrivals):
        slabs = sum(count for _, _, count in group)
        right = arrived.reshape(slabs, virtuals, virtuals)
        ct = jnp.swapaxes(right, 1, 2).reshape(slabs * virtuals, virtuals)
        at = 0
        for t, start, count in group:
            ladder_t = ladder_transposed(
                ct[at * virtuals:(at + count) * virtuals], tts[t],
                bq[t, start:start + count], ladder_t,
            )
            at += count
    ladder_sum = ladder_t.T
    vert = lax.axis_size("vert")
    slab_width = virtuals // vert
    ladder = lax.all_to_all(
        ladder_sum.reshape(vert, slab_width, -1), "vert", 0, 0, tiled=True
    ).sum(0)
    offset = lax.axis_index("vert") * slab_width
    labels = jnp.arange(kpoints, dtype=jnp.int32)
    owner_index = lax.axis_index("ka")
    momentum_b = jnp.sum(jnp.where(labels == owner_index, kb_table, 0))
    energy_rows = jnp.sum(jnp.where((labels == owner_index)[:, None], vir_energy, 0.0), axis=0)
    energy_other = jnp.sum(jnp.where((labels == momentum_b)[:, None], vir_energy, 0.0), axis=0)
    energy_a = lax.dynamic_slice_in_dim(energy_rows, offset, slab_width, 0)
    own_rows = lax.dynamic_slice_in_dim(own_block, offset, slab_width, 0).astype(jnp.float32)
    own_rows = own_rows.reshape(slab_width, pair_count, virtuals)
    shift_energy = (
        energy_a[:, None, None] + energy_other[None, None, :] - pair_energy[None, :, None]
    )
    combined = ladder + (shift_energy * own_rows).reshape(slab_width, pair_count * virtuals)
    return combined.astype(jnp.bfloat16)[None]


def solution(mesh):
    in_specs = (
        P("ka", None, None),
        P("ka", None, "vert", None),
        P(None, None, "vert", "ka"),
        P(),
        P(),
        P(),
    )
    out_specs = P("ka", "vert", None)
    return jax.shard_map(shards, mesh=mesh, in_specs=in_specs, out_specs=out_specs, check_vma=False)
```

```python
import functools

import jax
import jax.numpy as jnp
from jax import lax
from jax.experimental import pallas as pl
from jax.experimental.pallas import tpu as pltpu
from jax.sharding import PartitionSpec as P


def shifted(value, axis, steps):
    count = lax.axis_size(axis)
    pairs = [(source, (source + steps) % count) for source in range(count)]
    return lax.ppermute(value, axis, pairs)


def ladder_kernel(ct_ref, tt_ref, b_ref, acc_ref, out_ref, *, chunk, nv, pairs, lanes):
    j = pl.program_id(0)

    @pl.when(j == 0)
    def _():
        out_ref[...] = acc_ref[...]

    half = jnp.dot(ct_ref[...], tt_ref[...], preferred_element_type=jnp.float32)
    half = half.astype(jnp.bfloat16)
    acc = out_ref[...]
    for l in range(chunk):
        rows = half[l * nv:(l + 1) * nv]
        stacked = jnp.concatenate(
            [rows[:, p * lanes:p * lanes + nv] for p in range(pairs)], axis=0
        )
        acc = acc + lax.dot_general(
            stacked, b_ref[l], (((1,), (1,)), ((), ())),
            preferred_element_type=jnp.float32,
        )
    out_ref[...] = acc


def ladder_transposed(ct, tt, bq, acc, chunk=8):
    rows, nv = ct.shape
    aux = bq.shape[0]
    lanes = 128
    pairs = tt.shape[1] // lanes
    steps = aux // chunk
    kernel = functools.partial(ladder_kernel, chunk=chunk, nv=nv, pairs=pairs, lanes=lanes)
    flops = 2 * aux * nv * nv * (pairs * lanes + pairs * nv)
    return pl.pallas_call(
        kernel,
        out_shape=jax.ShapeDtypeStruct((pairs * nv, nv), jnp.float32),
        grid=(steps,),
        in_specs=[
            pl.BlockSpec((chunk * nv, nv), lambda j: (j, 0)),
            pl.BlockSpec((nv, pairs * lanes), lambda j: (0, 0)),
            pl.BlockSpec((chunk, nv, nv), lambda j: (j, 0, 0)),
            pl.BlockSpec((pairs * nv, nv), lambda j: (0, 0)),
        ],
        out_specs=pl.BlockSpec((pairs * nv, nv), lambda j: (0, 0)),
        input_output_aliases={3: 0},
        compiler_params=pltpu.CompilerParams(
            dimension_semantics=("arbitrary",),
            vmem_limit_bytes=48 * 1024 * 1024,
        ),
        cost_estimate=pl.CostEstimate(
            flops=flops, transcendentals=0,
            bytes_accessed=2 * (ct.size + tt.size + bq.size) + 8 * pairs * nv * nv,
        ),
    )(ct, tt, bq, acc)


def trial_transposed(block, virtuals, pair_count):
    t = block.reshape(virtuals, pair_count, virtuals)
    t = jnp.transpose(t, (2, 1, 0))
    t = jnp.pad(t, ((0, 0), (0, 0), (0, 128 - virtuals)))
    return t.reshape(virtuals, pair_count * 128)


def shards(trial_vector, left_factor, right_factor, kb_table, vir_energy, pair_energy):
    kpoints = vir_energy.shape[0]
    virtuals = vir_energy.shape[1]
    transfers = left_factor.shape[1]
    aux_local = left_factor.shape[2]
    pair_count = trial_vector.shape[2] // virtuals
    own_block = trial_vector[0]
    bq = left_factor[0].reshape(transfers, aux_local, virtuals, virtuals)
    blocks = [own_block] + [
        shifted(trial_vector, "ka", transfer)[0] for transfer in range(1, transfers)
    ]
    tail = aux_local // 2
    last = transfers - 1
    groups = [
        [(t, 0, aux_local) for t in range(last)] + [(last, 0, aux_local - tail)],
        [(last, aux_local - tail, tail)],
    ]
    arrivals = []
    for group in groups:
        piece = jnp.concatenate(
            [right_factor[:, t, start:start + count] for t, start, count in group], axis=1
        )
        piece = piece.at[kb_table].get(mode="promise_in_bounds")
        if arrivals:
            piece, arrivals[-1], bq, blocks = lax.optimization_barrier(
                (piece, arrivals[-1], bq, blocks)
            )
        arrivals.append(
            lax.all_to_all(piece, "ka", split_axis=0, concat_axis=2, tiled=True)[0]
        )
    ladder_t = jnp.zeros((pair_count * virtuals, virtuals), jnp.float32)
    tts = [trial_transposed(b, virtuals, pair_count) for b in blocks]
    for group, arrived in zip(groups, arrivals):
        slabs = sum(count for _, _, count in group)
        right = arrived.reshape(slabs, virtuals, virtuals)
        ct = jnp.swapaxes(right, 1, 2).reshape(slabs * virtuals, virtuals)
        at = 0
        for t, start, count in group:
            ladder_t = ladder_transposed(
                ct[at * virtuals:(at + count) * virtuals], tts[t],
                bq[t, start:start + count], ladder_t,
            )
            at += count
    ladder_sum = ladder_t.T
    vert = lax.axis_size("vert")
    slab_width = virtuals // vert
    slabs = ladder_sum.reshape(vert, slab_width, -1)
    me = lax.axis_index("vert")
    ladder = lax.dynamic_index_in_dim(slabs, me, 0, keepdims=False)
    for step in range(1, vert):
        outgoing = lax.dynamic_index_in_dim(slabs, (me + step) % vert, 0, keepdims=False)
        ladder = ladder + shifted(outgoing, "vert", step)
    offset = lax.axis_index("vert") * slab_width
    labels = jnp.arange(kpoints, dtype=jnp.int32)
    owner_index = lax.axis_index("ka")
    momentum_b = jnp.sum(jnp.where(labels == owner_index, kb_table, 0))
    energy_rows = jnp.sum(jnp.where((labels == owner_index)[:, None], vir_energy, 0.0), axis=0)
    energy_other = jnp.sum(jnp.where((labels == momentum_b)[:, None], vir_energy, 0.0), axis=0)
    energy_a = lax.dynamic_slice_in_dim(energy_rows, offset, slab_width, 0)
    own_rows = lax.dynamic_slice_in_dim(own_block, offset, slab_width, 0).astype(jnp.float32)
    own_rows = own_rows.reshape(slab_width, pair_count, virtuals)
    shift_energy = (
        energy_a[:, None, None] + energy_other[None, None, :] - pair_energy[None, :, None]
    )
    combined = ladder + (shift_energy * own_rows).reshape(slab_width, pair_count * virtuals)
    return combined.astype(jnp.bfloat16)[None]


def solution(mesh):
    in_specs = (
        P("ka", None, None),
        P("ka", None, "vert", None),
        P(None, None, "vert", "ka"),
        P(),
        P(),
        P(),
    )
    out_specs = P("ka", "vert", None)
    return jax.shard_map(shards, mesh=mesh, in_specs=in_specs, out_specs=out_specs, check_vma=False)
```

```python
import functools

import jax
import jax.numpy as jnp
from jax import lax
from jax.experimental import pallas as pl
from jax.experimental.pallas import tpu as pltpu
from jax.sharding import PartitionSpec as P


def shifted(value, axis, steps):
    count = lax.axis_size(axis)
    pairs = [(source, (source + steps) % count) for source in range(count)]
    return lax.ppermute(value, axis, pairs)


def ladder_kernel(ct_ref, tt_ref, b_ref, acc_ref, out_ref, *, chunk, nv, pairs, lanes):
    j = pl.program_id(0)

    @pl.when(j == 0)
    def _():
        out_ref[...] = acc_ref[...]

    half = jnp.dot(ct_ref[...], tt_ref[...], preferred_element_type=jnp.float32)
    half = half.astype(jnp.bfloat16)
    acc = out_ref[...]
    for two in range(chunk // 2):
        stacked = []
        for l in (2 * two, 2 * two + 1):
            rows = half[l * nv:(l + 1) * nv]
            stacked.append(jnp.concatenate(
                [rows[:, p * lanes:(p + 1) * lanes] for p in range(pairs)], axis=0
            ))
        acc = acc + lax.dot_general(
            jnp.concatenate(stacked, axis=1), b_ref[two], (((1,), (1,)), ((), ())),
            preferred_element_type=jnp.float32,
        )
    out_ref[...] = acc


def ladder_transposed(ct, tt, bpair, acc, chunk=8):
    rows, nv = ct.shape
    aux = 2 * bpair.shape[0]
    lanes = 128
    pairs = tt.shape[1] // lanes
    steps = aux // chunk
    kernel = functools.partial(ladder_kernel, chunk=chunk, nv=nv, pairs=pairs, lanes=lanes)
    flops = 2 * aux * nv * nv * (pairs * lanes + pairs * nv)
    return pl.pallas_call(
        kernel,
        out_shape=jax.ShapeDtypeStruct((pairs * nv, nv), jnp.float32),
        grid=(steps,),
        in_specs=[
            pl.BlockSpec((chunk * nv, nv), lambda j: (j, 0)),
            pl.BlockSpec((nv, pairs * lanes), lambda j: (0, 0)),
            pl.BlockSpec((chunk // 2, nv, 2 * lanes), lambda j: (j, 0, 0)),
            pl.BlockSpec((pairs * nv, nv), lambda j: (0, 0)),
        ],
        out_specs=pl.BlockSpec((pairs * nv, nv), lambda j: (0, 0)),
        input_output_aliases={3: 0},
        compiler_params=pltpu.CompilerParams(
            dimension_semantics=("arbitrary",),
            vmem_limit_bytes=48 * 1024 * 1024,
        ),
        cost_estimate=pl.CostEstimate(
            flops=flops, transcendentals=0,
            bytes_accessed=2 * (ct.size + tt.size + bpair.size) + 8 * pairs * nv * nv,
        ),
    )(ct, tt, bpair, acc)


def left_pairs(left, virtuals):
    transfers, aux = left.shape[0], left.shape[1]
    b = left.reshape(transfers, aux // 2, 2, virtuals, virtuals)
    b = jnp.pad(b, ((0, 0), (0, 0), (0, 0), (0, 0), (0, 128 - virtuals)))
    b = jnp.transpose(b, (0, 1, 3, 2, 4))
    return b.reshape(transfers, aux // 2, virtuals, 256)


def trial_transposed(block, virtuals, pair_count):
    t = block.reshape(virtuals, pair_count, virtuals)
    t = jnp.transpose(t, (2, 1, 0))
    t = jnp.pad(t, ((0, 0), (0, 0), (0, 128 - virtuals)))
    return t.reshape(virtuals, pair_count * 128)


def shards(trial_vector, left_factor, right_factor, kb_table, vir_energy, pair_energy):
    kpoints = vir_energy.shape[0]
    virtuals = vir_energy.shape[1]
    transfers = left_factor.shape[1]
    aux_local = left_factor.shape[2]
    pair_count = trial_vector.shape[2] // virtuals
    own_block = trial_vector[0]
    bq = left_pairs(left_factor[0], virtuals)
    blocks = [own_block] + [
        shifted(trial_vector, "ka", transfer)[0] for transfer in range(1, transfers)
    ]
    tail = aux_local // 2
    last = transfers - 1
    groups = [
        [(t, 0, aux_local) for t in range(last)] + [(last, 0, aux_local - tail)],
        [(last, aux_local - tail, tail)],
    ]
    arrivals = []
    for group in groups:
        piece = jnp.concatenate(
            [right_factor[:, t, start:start + count] for t, start, count in group], axis=1
        )
        piece = piece.at[kb_table].get(mode="promise_in_bounds")
        if arrivals:
            piece, arrivals[-1], bq, blocks = lax.optimization_barrier(
                (piece, arrivals[-1], bq, blocks)
            )
        arrivals.append(
            lax.all_to_all(piece, "ka", split_axis=0, concat_axis=2, tiled=True)[0]
        )
    ladder_t = jnp.zeros((pair_count * virtuals, virtuals), jnp.float32)
    tts = [trial_transposed(b, virtuals, pair_count) for b in blocks]
    for group, arrived in zip(groups, arrivals):
        slabs = sum(count for _, _, count in group)
        right = arrived.reshape(slabs, virtuals, virtuals)
        ct = jnp.swapaxes(right, 1, 2).reshape(slabs * virtuals, virtuals)
        at = 0
        for t, start, count in group:
            ladder_t = ladder_transposed(
                ct[at * virtuals:(at + count) * virtuals], tts[t],
                bq[t, start // 2:(start + count) // 2], ladder_t,
            )
            at += count
    ladder_sum = ladder_t.T
    vert = lax.axis_size("vert")
    slab_width = virtuals // vert
    ladder = lax.all_to_all(
        ladder_sum.reshape(vert, slab_width, -1), "vert", 0, 0, tiled=True
    ).sum(0)
    offset = lax.axis_index("vert") * slab_width
    labels = jnp.arange(kpoints, dtype=jnp.int32)
    owner_index = lax.axis_index("ka")
    momentum_b = jnp.sum(jnp.where(labels == owner_index, kb_table, 0))
    energy_rows = jnp.sum(jnp.where((labels == owner_index)[:, None], vir_energy, 0.0), axis=0)
    energy_other = jnp.sum(jnp.where((labels == momentum_b)[:, None], vir_energy, 0.0), axis=0)
    energy_a = lax.dynamic_slice_in_dim(energy_rows, offset, slab_width, 0)
    own_rows = lax.dynamic_slice_in_dim(own_block, offset, slab_width, 0).astype(jnp.float32)
    own_rows = own_rows.reshape(slab_width, pair_count, virtuals)
    shift_energy = (
        energy_a[:, None, None] + energy_other[None, None, :] - pair_energy[None, :, None]
    )
    combined = ladder + (shift_energy * own_rows).reshape(slab_width, pair_count * virtuals)
    return combined.astype(jnp.bfloat16)[None]


def solution(mesh):
    in_specs = (
        P("ka", None, None),
        P("ka", None, "vert", None),
        P(None, None, "vert", "ka"),
        P(),
        P(),
        P(),
    )
    out_specs = P("ka", "vert", None)
    return jax.shard_map(shards, mesh=mesh, in_specs=in_specs, out_specs=out_specs, check_vma=False)
```

```python
import functools

import jax
import jax.numpy as jnp
from jax import lax
from jax.experimental import pallas as pl
from jax.experimental.pallas import tpu as pltpu
from jax.sharding import PartitionSpec as P


def shifted(value, axis, steps):
    count = lax.axis_size(axis)
    pairs = [(source, (source + steps) % count) for source in range(count)]
    return lax.ppermute(value, axis, pairs)


def ladder_kernel(ct_ref, tt_ref, b_ref, acc_ref, out_ref, *, chunk, nv, pairs, lanes):
    j = pl.program_id(0)

    @pl.when(j == 0)
    def _():
        out_ref[...] = acc_ref[...]

    half = jnp.dot(ct_ref[...], tt_ref[...], preferred_element_type=jnp.float32)
    half = half.astype(jnp.bfloat16)
    acc = out_ref[...]
    for two in range(chunk // 2):
        stacked = []
        for l in (2 * two, 2 * two + 1):
            rows = half[l * nv:(l + 1) * nv]
            stacked.append(jnp.concatenate(
                [rows[:, p * lanes:(p + 1) * lanes] for p in range(pairs)], axis=0
            ))
        acc = acc + lax.dot_general(
            jnp.concatenate(stacked, axis=1), b_ref[two], (((1,), (1,)), ((), ())),
            preferred_element_type=jnp.float32,
        )
    out_ref[...] = acc


def ladder_transposed(ct, tt, bpair, acc, chunk=8):
    rows, nv = ct.shape
    aux = 2 * bpair.shape[0]
    lanes = 128
    pairs = tt.shape[1] // lanes
    steps = aux // chunk
    kernel = functools.partial(ladder_kernel, chunk=chunk, nv=nv, pairs=pairs, lanes=lanes)
    flops = 2 * aux * nv * nv * (pairs * lanes + pairs * nv)
    return pl.pallas_call(
        kernel,
        out_shape=jax.ShapeDtypeStruct((pairs * nv, nv), jnp.float32),
        grid=(steps,),
        in_specs=[
            pl.BlockSpec((chunk * nv, nv), lambda j: (j, 0)),
            pl.BlockSpec((nv, pairs * lanes), lambda j: (0, 0)),
            pl.BlockSpec((chunk // 2, nv, 2 * lanes), lambda j: (j, 0, 0)),
            pl.BlockSpec((pairs * nv, nv), lambda j: (0, 0)),
        ],
        out_specs=pl.BlockSpec((pairs * nv, nv), lambda j: (0, 0)),
        input_output_aliases={3: 0},
        compiler_params=pltpu.CompilerParams(
            dimension_semantics=("arbitrary",),
            vmem_limit_bytes=48 * 1024 * 1024,
        ),
        cost_estimate=pl.CostEstimate(
            flops=flops, transcendentals=0,
            bytes_accessed=2 * (ct.size + tt.size + bpair.size) + 8 * pairs * nv * nv,
        ),
    )(ct, tt, bpair, acc)


def left_pairs(left, virtuals):
    transfers, aux = left.shape[0], left.shape[1]
    b = left.reshape(transfers, aux // 2, 2, virtuals, virtuals)
    b = jnp.pad(b, ((0, 0), (0, 0), (0, 0), (0, 0), (0, 128 - virtuals)))
    b = jnp.transpose(b, (0, 1, 3, 2, 4))
    return b.reshape(transfers, aux // 2, virtuals, 256)


def trial_transposed(block, virtuals, pair_count):
    t = block.reshape(virtuals, pair_count, virtuals)
    t = jnp.transpose(t, (2, 1, 0))
    t = jnp.pad(t, ((0, 0), (0, 0), (0, 128 - virtuals)))
    return t.reshape(virtuals, pair_count * 128)


def shards(trial_vector, left_factor, right_factor, kb_table, vir_energy, pair_energy):
    kpoints = vir_energy.shape[0]
    virtuals = vir_energy.shape[1]
    transfers = left_factor.shape[1]
    aux_local = left_factor.shape[2]
    pair_count = trial_vector.shape[2] // virtuals
    own_block = trial_vector[0]
    bq = left_pairs(left_factor[0], virtuals)
    blocks = [own_block] + [
        shifted(trial_vector, "ka", transfer)[0] for transfer in range(1, transfers)
    ]
    tail = aux_local // 2
    last = transfers - 1
    groups = [
        [(t, 0, aux_local) for t in range(last)] + [(last, 0, aux_local - tail)],
        [(last, aux_local - tail, tail)],
    ]
    arrivals = []
    for group in groups:
        piece = jnp.concatenate(
            [right_factor[:, t, start:start + count] for t, start, count in group], axis=1
        )
        piece = piece.at[kb_table].get(mode="promise_in_bounds")
        if arrivals:
            piece, arrivals[-1], bq = lax.optimization_barrier((piece, arrivals[-1], bq))
        else:
            piece, blocks = lax.optimization_barrier((piece, blocks))
        arrivals.append(
            lax.all_to_all(piece, "ka", split_axis=0, concat_axis=2, tiled=True)[0]
        )
    ladder_t = jnp.zeros((pair_count * virtuals, virtuals), jnp.float32)
    tts = [trial_transposed(b, virtuals, pair_count) for b in blocks]
    for group, arrived in zip(groups, arrivals):
        slabs = sum(count for _, _, count in group)
        right = arrived.reshape(slabs, virtuals, virtuals)
        ct = jnp.swapaxes(right, 1, 2).reshape(slabs * virtuals, virtuals)
        at = 0
        for t, start, count in group:
            ladder_t = ladder_transposed(
                ct[at * virtuals:(at + count) * virtuals], tts[t],
                bq[t, start // 2:(start + count) // 2], ladder_t,
            )
            at += count
    ladder_sum = ladder_t.T
    vert = lax.axis_size("vert")
    slab_width = virtuals // vert
    ladder = lax.all_to_all(
        ladder_sum.reshape(vert, slab_width, -1), "vert", 0, 0, tiled=True
    ).sum(0)
    offset = lax.axis_index("vert") * slab_width
    labels = jnp.arange(kpoints, dtype=jnp.int32)
    owner_index = lax.axis_index("ka")
    momentum_b = jnp.sum(jnp.where(labels == owner_index, kb_table, 0))
    energy_rows = jnp.sum(jnp.where((labels == owner_index)[:, None], vir_energy, 0.0), axis=0)
    energy_other = jnp.sum(jnp.where((labels == momentum_b)[:, None], vir_energy, 0.0), axis=0)
    energy_a = lax.dynamic_slice_in_dim(energy_rows, offset, slab_width, 0)
    own_rows = lax.dynamic_slice_in_dim(own_block, offset, slab_width, 0).astype(jnp.float32)
    own_rows = own_rows.reshape(slab_width, pair_count, virtuals)
    shift_energy = (
        energy_a[:, None, None] + energy_other[None, None, :] - pair_energy[None, :, None]
    )
    combined = ladder + (shift_energy * own_rows).reshape(slab_width, pair_count * virtuals)
    return combined.astype(jnp.bfloat16)[None]


def solution(mesh):
    in_specs = (
        P("ka", None, None),
        P("ka", None, "vert", None),
        P(None, None, "vert", "ka"),
        P(),
        P(),
        P(),
    )
    out_specs = P("ka", "vert", None)
    return jax.shard_map(shards, mesh=mesh, in_specs=in_specs, out_specs=out_specs, check_vma=False)
```

```python
import functools

import jax
import jax.numpy as jnp
from jax import lax
from jax.experimental import pallas as pl
from jax.experimental.pallas import tpu as pltpu
from jax.sharding import PartitionSpec as P


def shifted(value, axis, steps):
    count = lax.axis_size(axis)
    pairs = [(source, (source + steps) % count) for source in range(count)]
    return lax.ppermute(value, axis, pairs)


def ladder_kernel(ct_ref, tt_ref, b_ref, acc_ref, out_ref, *, chunk, nv, pairs, lanes):
    j = pl.program_id(0)

    @pl.when(j == 0)
    def _():
        out_ref[...] = acc_ref[...]

    half = jnp.dot(ct_ref[...], tt_ref[...], preferred_element_type=jnp.float32)
    half = half.astype(jnp.bfloat16)
    acc = out_ref[...]
    for two in range(chunk // 2):
        stacked = []
        for l in (2 * two, 2 * two + 1):
            rows = half[l * nv:(l + 1) * nv]
            stacked.append(jnp.concatenate(
                [rows[:, p * lanes:(p + 1) * lanes] for p in range(pairs)], axis=0
            ))
        acc = acc + lax.dot_general(
            jnp.concatenate(stacked, axis=1), b_ref[two], (((1,), (1,)), ((), ())),
            preferred_element_type=jnp.float32,
        )
    out_ref[...] = acc


def ladder_transposed(ct, tt, bpair, acc, chunk=8):
    rows, nv = ct.shape
    aux = 2 * bpair.shape[0]
    lanes = 128
    pairs = tt.shape[1] // lanes
    steps = aux // chunk
    kernel = functools.partial(ladder_kernel, chunk=chunk, nv=nv, pairs=pairs, lanes=lanes)
    flops = 2 * aux * nv * nv * (pairs * lanes + pairs * nv)
    return pl.pallas_call(
        kernel,
        out_shape=jax.ShapeDtypeStruct((pairs * nv, nv), jnp.float32),
        grid=(steps,),
        in_specs=[
            pl.BlockSpec((chunk * nv, nv), lambda j: (j, 0)),
            pl.BlockSpec((nv, pairs * lanes), lambda j: (0, 0)),
            pl.BlockSpec((chunk // 2, nv, 2 * lanes), lambda j: (j, 0, 0)),
            pl.BlockSpec((pairs * nv, nv), lambda j: (0, 0)),
        ],
        out_specs=pl.BlockSpec((pairs * nv, nv), lambda j: (0, 0)),
        input_output_aliases={3: 0},
        compiler_params=pltpu.CompilerParams(
            dimension_semantics=("arbitrary",),
            vmem_limit_bytes=48 * 1024 * 1024,
        ),
        cost_estimate=pl.CostEstimate(
            flops=flops, transcendentals=0,
            bytes_accessed=2 * (ct.size + tt.size + bpair.size) + 8 * pairs * nv * nv,
        ),
    )(ct, tt, bpair, acc)


def left_pairs(left, virtuals):
    transfers, aux = left.shape[0], left.shape[1]
    b = left.reshape(transfers, aux // 2, 2, virtuals, virtuals)
    b = jnp.pad(b, ((0, 0), (0, 0), (0, 0), (0, 0), (0, 128 - virtuals)))
    b = jnp.transpose(b, (0, 1, 3, 2, 4))
    return b.reshape(transfers, aux // 2, virtuals, 256)


def trial_transposed(block, virtuals, pair_count):
    t = block.reshape(virtuals, pair_count, virtuals)
    t = jnp.transpose(t, (2, 1, 0))
    t = jnp.pad(t, ((0, 0), (0, 0), (0, 128 - virtuals)))
    return t.reshape(virtuals, pair_count * 128)


def shards(trial_vector, left_factor, right_factor, kb_table, vir_energy, pair_energy):
    kpoints = vir_energy.shape[0]
    virtuals = vir_energy.shape[1]
    transfers = left_factor.shape[1]
    aux_local = left_factor.shape[2]
    pair_count = trial_vector.shape[2] // virtuals
    own_block = trial_vector[0]
    bq = left_pairs(left_factor[0], virtuals)
    blocks = [own_block] + [
        shifted(trial_vector, "ka", transfer)[0] for transfer in range(1, transfers)
    ]
    tail = aux_local // 2
    last = transfers - 1
    groups = [
        [(t, 0, aux_local) for t in range(last)] + [(last, 0, aux_local - tail)],
        [(last, aux_local - tail, tail)],
    ]
    arrivals = []
    for group in groups:
        piece = jnp.concatenate(
            [right_factor[:, t, start:start + count] for t, start, count in group], axis=1
        )
        piece = piece.at[kb_table].get(mode="promise_in_bounds")
        if arrivals:
            piece, arrivals[-1], bq, blocks = lax.optimization_barrier(
                (piece, arrivals[-1], bq, blocks)
            )
        arrivals.append(
            lax.all_to_all(piece, "ka", split_axis=0, concat_axis=2, tiled=True)[0]
        )
    ladder_t = jnp.zeros((pair_count * virtuals, virtuals), jnp.float32)
    tts = [trial_transposed(b, virtuals, pair_count) for b in blocks]
    for group, arrived in zip(groups, arrivals):
        slabs = sum(count for _, _, count in group)
        right = arrived.reshape(slabs, virtuals, virtuals)
        ct = jnp.swapaxes(right, 1, 2).reshape(slabs * virtuals, virtuals)
        at = 0
        for t, start, count in group:
            ladder_t = ladder_transposed(
                ct[at * virtuals:(at + count) * virtuals], tts[t],
                bq[t, start // 2:(start + count) // 2], ladder_t,
            )
            at += count
    ladder_sum = ladder_t.T
    vert = lax.axis_size(("zl", "core"))
    slab_width = virtuals // vert
    cores = lax.axis_size("core")
    stacked = ladder_sum.reshape(vert // cores, cores, slab_width, -1)
    stacked = lax.all_to_all(stacked, "core", 1, 1, tiled=True).sum(1)
    ladder = lax.all_to_all(stacked, "zl", 0, 0, tiled=True).sum(0)
    offset = lax.axis_index(("zl", "core")) * slab_width
    labels = jnp.arange(kpoints, dtype=jnp.int32)
    owner_index = lax.axis_index("ka")
    momentum_b = jnp.sum(jnp.where(labels == owner_index, kb_table, 0))
    energy_rows = jnp.sum(jnp.where((labels == owner_index)[:, None], vir_energy, 0.0), axis=0)
    energy_other = jnp.sum(jnp.where((labels == momentum_b)[:, None], vir_energy, 0.0), axis=0)
    energy_a = lax.dynamic_slice_in_dim(energy_rows, offset, slab_width, 0)
    own_rows = lax.dynamic_slice_in_dim(own_block, offset, slab_width, 0).astype(jnp.float32)
    own_rows = own_rows.reshape(slab_width, pair_count, virtuals)
    shift_energy = (
        energy_a[:, None, None] + energy_other[None, None, :] - pair_energy[None, :, None]
    )
    combined = ladder + (shift_energy * own_rows).reshape(slab_width, pair_count * virtuals)
    return combined.astype(jnp.bfloat16)[None]


def solution(mesh):
    kpoints, vert = mesh.devices.shape
    cores = 2
    split = jax.sharding.Mesh(
        mesh.devices.reshape(kpoints, vert // cores, cores), ("ka", "zl", "core")
    )
    slab = ("zl", "core")
    in_specs = (
        P("ka", None, None),
        P("ka", None, slab, None),
        P(None, None, slab, "ka"),
        P(),
        P(),
        P(),
    )
    out_specs = P("ka", slab, None)
    return jax.shard_map(shards, mesh=split, in_specs=in_specs, out_specs=out_specs, check_vma=False)
```

```python
import functools

import jax
import jax.numpy as jnp
from jax import lax
from jax.experimental import pallas as pl
from jax.experimental.pallas import tpu as pltpu
from jax.sharding import PartitionSpec as P


def shifted(value, axis, steps):
    count = lax.axis_size(axis)
    pairs = [(source, (source + steps) % count) for source in range(count)]
    return lax.ppermute(value, axis, pairs)


def ladder_kernel(ct_ref, tt_ref, b_ref, acc_ref, out_ref, *, chunk, nv, pairs, lanes):
    j = pl.program_id(0)

    @pl.when(j == 0)
    def _():
        out_ref[...] = acc_ref[...]

    half = jnp.dot(ct_ref[...], tt_ref[...], preferred_element_type=jnp.float32)
    half = half.astype(jnp.bfloat16)
    acc = out_ref[...]
    for two in range(chunk // 2):
        stacked = []
        for l in (2 * two, 2 * two + 1):
            rows = half[l * nv:(l + 1) * nv]
            stacked.append(jnp.concatenate(
                [rows[:, p * lanes:(p + 1) * lanes] for p in range(pairs)], axis=0
            ))
        acc = acc + lax.dot_general(
            jnp.concatenate(stacked, axis=1), b_ref[two], (((1,), (1,)), ((), ())),
            preferred_element_type=jnp.float32,
        )
    out_ref[...] = acc


def ladder_transposed(ct, tt, bpair, acc, chunk=8):
    rows, nv = ct.shape
    aux = 2 * bpair.shape[0]
    lanes = 128
    pairs = tt.shape[1] // lanes
    steps = aux // chunk
    kernel = functools.partial(ladder_kernel, chunk=chunk, nv=nv, pairs=pairs, lanes=lanes)
    flops = 2 * aux * nv * nv * (pairs * lanes + pairs * nv)
    return pl.pallas_call(
        kernel,
        out_shape=jax.ShapeDtypeStruct((pairs * nv, nv), jnp.float32),
        grid=(steps,),
        in_specs=[
            pl.BlockSpec((chunk * nv, nv), lambda j: (j, 0)),
            pl.BlockSpec((nv, pairs * lanes), lambda j: (0, 0)),
            pl.BlockSpec((chunk // 2, nv, 2 * lanes), lambda j: (j, 0, 0)),
            pl.BlockSpec((pairs * nv, nv), lambda j: (0, 0)),
        ],
        out_specs=pl.BlockSpec((pairs * nv, nv), lambda j: (0, 0)),
        input_output_aliases={3: 0},
        compiler_params=pltpu.CompilerParams(
            dimension_semantics=("arbitrary",),
            vmem_limit_bytes=48 * 1024 * 1024,
        ),
        cost_estimate=pl.CostEstimate(
            flops=flops, transcendentals=0,
            bytes_accessed=2 * (ct.size + tt.size + bpair.size) + 8 * pairs * nv * nv,
        ),
    )(ct, tt, bpair, acc)


def left_pairs(left, virtuals):
    transfers, aux = left.shape[0], left.shape[1]
    b = left.reshape(transfers, aux // 2, 2, virtuals, virtuals)
    b = jnp.pad(b, ((0, 0), (0, 0), (0, 0), (0, 0), (0, 128 - virtuals)))
    b = jnp.transpose(b, (0, 1, 3, 2, 4))
    return b.reshape(transfers, aux // 2, virtuals, 256)


def trial_transposed(block, virtuals, pair_count):
    t = block.reshape(virtuals, pair_count, virtuals)
    t = jnp.transpose(t, (2, 1, 0))
    t = jnp.pad(t, ((0, 0), (0, 0), (0, 128 - virtuals)))
    return t.reshape(virtuals, pair_count * 128)


def shards(trial_vector, left_factor, right_factor, kb_table, vir_energy, pair_energy):
    kpoints = vir_energy.shape[0]
    virtuals = vir_energy.shape[1]
    transfers = left_factor.shape[1]
    aux_local = left_factor.shape[2]
    pair_count = trial_vector.shape[2] // virtuals
    own_block = trial_vector[0]
    vert = lax.axis_size(("zl", "core"))
    slab_width = virtuals // vert
    offset = lax.axis_index(("zl", "core")) * slab_width
    labels = jnp.arange(kpoints, dtype=jnp.int32)
    owner_index = lax.axis_index("ka")
    momentum_b = jnp.sum(jnp.where(labels == owner_index, kb_table, 0))
    energy_rows = jnp.sum(jnp.where((labels == owner_index)[:, None], vir_energy, 0.0), axis=0)
    energy_other = jnp.sum(jnp.where((labels == momentum_b)[:, None], vir_energy, 0.0), axis=0)
    energy_a = lax.dynamic_slice_in_dim(energy_rows, offset, slab_width, 0)
    own_rows = lax.dynamic_slice_in_dim(own_block, offset, slab_width, 0).astype(jnp.float32)
    own_rows = own_rows.reshape(slab_width, pair_count, virtuals)
    shift_energy = (
        energy_a[:, None, None] + energy_other[None, None, :] - pair_energy[None, :, None]
    )
    orbital = (shift_energy * own_rows).reshape(slab_width, pair_count * virtuals)
    bq = left_pairs(left_factor[0], virtuals)
    blocks = [own_block] + [
        shifted(trial_vector, "ka", transfer)[0] for transfer in range(1, transfers)
    ]
    tail = aux_local // 2
    last = transfers - 1
    groups = [
        [(t, 0, aux_local) for t in range(last)] + [(last, 0, aux_local - tail)],
        [(last, aux_local - tail, tail)],
    ]
    arrivals = []
    for group in groups:
        piece = jnp.concatenate(
            [right_factor[:, t, start:start + count] for t, start, count in group], axis=1
        )
        piece = piece.at[kb_table].get(mode="promise_in_bounds")
        if arrivals:
            piece, arrivals[-1], bq, blocks, orbital = lax.optimization_barrier(
                (piece, arrivals[-1], bq, blocks, orbital)
            )
        arrivals.append(
            lax.all_to_all(piece, "ka", split_axis=0, concat_axis=2, tiled=True)[0]
        )
    ladder_t = jnp.zeros((pair_count * virtuals, virtuals), jnp.float32)
    tts = [trial_transposed(b, virtuals, pair_count) for b in blocks]
    for group, arrived in zip(groups, arrivals):
        slabs = sum(count for _, _, count in group)
        right = arrived.reshape(slabs, virtuals, virtuals)
        ct = jnp.swapaxes(right, 1, 2).reshape(slabs * virtuals, virtuals)
        at = 0
        for t, start, count in group:
            ladder_t = ladder_transposed(
                ct[at * virtuals:(at + count) * virtuals], tts[t],
                bq[t, start // 2:(start + count) // 2], ladder_t,
            )
            at += count
    ladder_sum = ladder_t.T
    cores = lax.axis_size("core")
    stacked = ladder_sum.reshape(vert // cores, cores, slab_width, -1)
    stacked = lax.all_to_all(stacked, "core", 1, 1, tiled=True).sum(1)
    ladder = lax.all_to_all(stacked, "zl", 0, 0, tiled=True).sum(0)
    combined = ladder + orbital
    return combined.astype(jnp.bfloat16)[None]


def solution(mesh):
    kpoints, vert = mesh.devices.shape
    cores = 2
    split = jax.sharding.Mesh(
        mesh.devices.reshape(kpoints, vert // cores, cores), ("ka", "zl", "core")
    )
    slab = ("zl", "core")
    in_specs = (
        P("ka", None, None),
        P("ka", None, slab, None),
        P(None, None, slab, "ka"),
        P(),
        P(),
        P(),
    )
    out_specs = P("ka", slab, None)
    return jax.shard_map(shards, mesh=split, in_specs=in_specs, out_specs=out_specs, check_vma=False)
```

```python
import functools

import jax
import jax.numpy as jnp
from jax import lax
from jax.experimental import pallas as pl
from jax.experimental.pallas import tpu as pltpu
from jax.sharding import PartitionSpec as P


def shifted(value, axis, steps):
    count = lax.axis_size(axis)
    pairs = [(source, (source + steps) % count) for source in range(count)]
    return lax.ppermute(value, axis, pairs)


def ladder_kernel(ct_ref, tt_ref, b_ref, acc_ref, out_ref, *, chunk, nv, pairs, lanes):
    j = pl.program_id(0)

    @pl.when(j == 0)
    def _():
        out_ref[...] = acc_ref[...]

    half = jnp.dot(ct_ref[...], tt_ref[...], preferred_element_type=jnp.float32)
    half = half.astype(jnp.bfloat16)
    acc = out_ref[...]
    for two in range(chunk // 2):
        stacked = []
        for l in (2 * two, 2 * two + 1):
            rows = half[l * nv:(l + 1) * nv]
            stacked.append(jnp.concatenate(
                [rows[:, p * lanes:(p + 1) * lanes] for p in range(pairs)], axis=0
            ))
        acc = acc + lax.dot_general(
            jnp.concatenate(stacked, axis=1), b_ref[two], (((1,), (1,)), ((), ())),
            preferred_element_type=jnp.float32,
        )
    out_ref[...] = acc


def ladder_transposed(ct, tt, bpair, acc, chunk=8):
    rows, nv = ct.shape
    aux = 2 * bpair.shape[0]
    lanes = 128
    pairs = tt.shape[1] // lanes
    steps = aux // chunk
    kernel = functools.partial(ladder_kernel, chunk=chunk, nv=nv, pairs=pairs, lanes=lanes)
    flops = 2 * aux * nv * nv * (pairs * lanes + pairs * nv)
    return pl.pallas_call(
        kernel,
        out_shape=jax.ShapeDtypeStruct((pairs * nv, nv), jnp.float32),
        grid=(steps,),
        in_specs=[
            pl.BlockSpec((chunk * nv, nv), lambda j: (j, 0)),
            pl.BlockSpec((nv, pairs * lanes), lambda j: (0, 0)),
            pl.BlockSpec((chunk // 2, nv, 2 * lanes), lambda j: (j, 0, 0)),
            pl.BlockSpec((pairs * nv, nv), lambda j: (0, 0)),
        ],
        out_specs=pl.BlockSpec((pairs * nv, nv), lambda j: (0, 0)),
        input_output_aliases={3: 0},
        compiler_params=pltpu.CompilerParams(
            dimension_semantics=("arbitrary",),
            vmem_limit_bytes=48 * 1024 * 1024,
        ),
        cost_estimate=pl.CostEstimate(
            flops=flops, transcendentals=0,
            bytes_accessed=2 * (ct.size + tt.size + bpair.size) + 8 * pairs * nv * nv,
        ),
    )(ct, tt, bpair, acc)


def left_pairs(left, virtuals):
    transfers, aux = left.shape[0], left.shape[1]
    b = left.reshape(transfers, aux // 2, 2, virtuals, virtuals)
    b = jnp.pad(b, ((0, 0), (0, 0), (0, 0), (0, 0), (0, 128 - virtuals)))
    b = jnp.transpose(b, (0, 1, 3, 2, 4))
    return b.reshape(transfers, aux // 2, virtuals, 256)


def trial_transposed(block, virtuals, pair_count):
    t = block.reshape(virtuals, pair_count, virtuals)
    t = jnp.transpose(t, (2, 1, 0))
    t = jnp.pad(t, ((0, 0), (0, 0), (0, 128 - virtuals)))
    return t.reshape(virtuals, pair_count * 128)


def shards(trial_vector, left_factor, right_factor, kb_table, vir_energy, pair_energy):
    kpoints = vir_energy.shape[0]
    virtuals = vir_energy.shape[1]
    transfers = left_factor.shape[1]
    aux_local = left_factor.shape[2]
    pair_count = trial_vector.shape[2] // virtuals
    own_block = trial_vector[0]
    vert = lax.axis_size(("zl", "core"))
    slab_width = virtuals // vert
    offset = lax.axis_index(("zl", "core")) * slab_width
    labels = jnp.arange(kpoints, dtype=jnp.int32)
    owner_index = lax.axis_index("ka")
    momentum_b = jnp.sum(jnp.where(labels == owner_index, kb_table, 0))
    energy_rows = jnp.sum(jnp.where((labels == owner_index)[:, None], vir_energy, 0.0), axis=0)
    energy_other = jnp.sum(jnp.where((labels == momentum_b)[:, None], vir_energy, 0.0), axis=0)
    energy_a = lax.dynamic_slice_in_dim(energy_rows, offset, slab_width, 0)
    own_rows = lax.dynamic_slice_in_dim(own_block, offset, slab_width, 0).astype(jnp.float32)
    own_rows = own_rows.reshape(slab_width, pair_count, virtuals)
    shift_energy = (
        energy_a[:, None, None] + energy_other[None, None, :] - pair_energy[None, :, None]
    )
    orbital = (shift_energy * own_rows).reshape(slab_width, pair_count * virtuals)
    bq = left_pairs(left_factor[0], virtuals)
    blocks = [own_block] + [
        shifted(trial_vector, "ka", transfer)[0] for transfer in range(1, transfers)
    ]
    tail = aux_local // 2
    last = transfers - 1
    groups = [
        [(t, 0, aux_local) for t in range(last)] + [(last, 0, aux_local - tail)],
        [(last, aux_local - tail, tail)],
    ]
    arrivals = []
    for group in groups:
        piece = jnp.concatenate(
            [right_factor[:, t, start:start + count] for t, start, count in group], axis=1
        )
        piece = piece.at[kb_table].get(mode="promise_in_bounds")
        if arrivals:
            piece, arrivals[-1], bq, orbital = lax.optimization_barrier(
                (piece, arrivals[-1], bq, orbital)
            )
        arrivals.append(
            lax.all_to_all(piece, "ka", split_axis=0, concat_axis=2, tiled=True)[0]
        )
    ladder_t = jnp.zeros((pair_count * virtuals, virtuals), jnp.float32)
    tts = [trial_transposed(b, virtuals, pair_count) for b in blocks]
    for group, arrived in zip(groups, arrivals):
        slabs = sum(count for _, _, count in group)
        right = arrived.reshape(slabs, virtuals, virtuals)
        ct = jnp.swapaxes(right, 1, 2).reshape(slabs * virtuals, virtuals)
        at = 0
        for t, start, count in group:
            ladder_t = ladder_transposed(
                ct[at * virtuals:(at + count) * virtuals], tts[t],
                bq[t, start // 2:(start + count) // 2], ladder_t,
            )
            at += count
    ladder_sum = ladder_t.T
    cores = lax.axis_size("core")
    stacked = ladder_sum.reshape(vert // cores, cores, slab_width, -1)
    stacked = lax.all_to_all(stacked, "core", 1, 1, tiled=True).sum(1)
    ladder = lax.all_to_all(stacked, "zl", 0, 0, tiled=True).sum(0)
    combined = ladder + orbital
    return combined.astype(jnp.bfloat16)[None]


def solution(mesh):
    kpoints, vert = mesh.devices.shape
    cores = 2
    split = jax.sharding.Mesh(
        mesh.devices.reshape(kpoints, vert // cores, cores), ("ka", "zl", "core")
    )
    slab = ("zl", "core")
    in_specs = (
        P("ka", None, None),
        P("ka", None, slab, None),
        P(None, None, slab, "ka"),
        P(),
        P(),
        P(),
    )
    out_specs = P("ka", slab, None)
    return jax.shard_map(shards, mesh=split, in_specs=in_specs, out_specs=out_specs, check_vma=False)
```

```python
import functools

import jax
import jax.numpy as jnp
from jax import lax
from jax.experimental import pallas as pl
from jax.experimental.pallas import tpu as pltpu
from jax.sharding import PartitionSpec as P


def shifted(value, axis, steps):
    count = lax.axis_size(axis)
    pairs = [(source, (source + steps) % count) for source in range(count)]
    return lax.ppermute(value, axis, pairs)


def ladder_kernel(ct_ref, tt_ref, b_ref, acc_ref, out_ref, *, chunk, nv, pairs, lanes):
    j = pl.program_id(0)

    @pl.when(j == 0)
    def _():
        out_ref[...] = acc_ref[...]

    half = jnp.dot(ct_ref[...], tt_ref[...], preferred_element_type=jnp.float32)
    half = half.astype(jnp.bfloat16)
    acc = out_ref[...]
    for two in range(chunk // 2):
        stacked = []
        for l in (2 * two, 2 * two + 1):
            rows = half[l * nv:(l + 1) * nv]
            stacked.append(jnp.concatenate(
                [rows[:, p * lanes:(p + 1) * lanes] for p in range(pairs)], axis=0
            ))
        acc = acc + lax.dot_general(
            jnp.concatenate(stacked, axis=1), b_ref[two], (((1,), (1,)), ((), ())),
            preferred_element_type=jnp.float32,
        )
    out_ref[...] = acc


def ladder_transposed(ct, tt, bpair, acc):
    rows, nv = ct.shape
    aux = 2 * bpair.shape[0]
    lanes = 128
    pairs = tt.shape[1] // lanes
    chunk = max(c for c in (8, 6, 4, 2) if aux % c == 0)
    steps = aux // chunk
    kernel = functools.partial(ladder_kernel, chunk=chunk, nv=nv, pairs=pairs, lanes=lanes)
    flops = 2 * aux * nv * nv * (pairs * lanes + pairs * nv)
    return pl.pallas_call(
        kernel,
        out_shape=jax.ShapeDtypeStruct((pairs * nv, nv), jnp.float32),
        grid=(steps,),
        in_specs=[
            pl.BlockSpec((chunk * nv, nv), lambda j: (j, 0)),
            pl.BlockSpec((nv, pairs * lanes), lambda j: (0, 0)),
            pl.BlockSpec((chunk // 2, nv, 2 * lanes), lambda j: (j, 0, 0)),
            pl.BlockSpec((pairs * nv, nv), lambda j: (0, 0)),
        ],
        out_specs=pl.BlockSpec((pairs * nv, nv), lambda j: (0, 0)),
        input_output_aliases={3: 0},
        compiler_params=pltpu.CompilerParams(
            dimension_semantics=("arbitrary",),
            vmem_limit_bytes=48 * 1024 * 1024,
        ),
        cost_estimate=pl.CostEstimate(
            flops=flops, transcendentals=0,
            bytes_accessed=2 * (ct.size + tt.size + bpair.size) + 8 * pairs * nv * nv,
        ),
    )(ct, tt, bpair, acc)


def left_pairs(left, virtuals):
    transfers, aux = left.shape[0], left.shape[1]
    b = left.reshape(transfers, aux // 2, 2, virtuals, virtuals)
    b = jnp.pad(b, ((0, 0), (0, 0), (0, 0), (0, 0), (0, 128 - virtuals)))
    b = jnp.transpose(b, (0, 1, 3, 2, 4))
    return b.reshape(transfers, aux // 2, virtuals, 256)


def trial_transposed(block, virtuals, pair_count):
    t = block.reshape(virtuals, pair_count, virtuals)
    t = jnp.transpose(t, (2, 1, 0))
    t = jnp.pad(t, ((0, 0), (0, 0), (0, 128 - virtuals)))
    return t.reshape(virtuals, pair_count * 128)


def shards(trial_vector, left_factor, right_factor, kb_table, vir_energy, pair_energy):
    kpoints = vir_energy.shape[0]
    virtuals = vir_energy.shape[1]
    transfers = left_factor.shape[1]
    aux_local = left_factor.shape[2]
    pair_count = trial_vector.shape[2] // virtuals
    own_block = trial_vector[0]
    vert = lax.axis_size(("zl", "core"))
    slab_width = virtuals // vert
    offset = lax.axis_index(("zl", "core")) * slab_width
    labels = jnp.arange(kpoints, dtype=jnp.int32)
    owner_index = lax.axis_index("ka")
    momentum_b = jnp.sum(jnp.where(labels == owner_index, kb_table, 0))
    energy_rows = jnp.sum(jnp.where((labels == owner_index)[:, None], vir_energy, 0.0), axis=0)
    energy_other = jnp.sum(jnp.where((labels == momentum_b)[:, None], vir_energy, 0.0), axis=0)
    energy_a = lax.dynamic_slice_in_dim(energy_rows, offset, slab_width, 0)
    own_rows = lax.dynamic_slice_in_dim(own_block, offset, slab_width, 0).astype(jnp.float32)
    own_rows = own_rows.reshape(slab_width, pair_count, virtuals)
    shift_energy = (
        energy_a[:, None, None] + energy_other[None, None, :] - pair_energy[None, :, None]
    )
    orbital = (shift_energy * own_rows).reshape(slab_width, pair_count * virtuals)
    bq = left_pairs(left_factor[0], virtuals)
    blocks = [own_block] + [
        shifted(trial_vector, "ka", transfer)[0] for transfer in range(1, transfers)
    ]
    tail = (3 * aux_local) // 8
    last = transfers - 1
    groups = [
        [(t, 0, aux_local) for t in range(last)] + [(last, 0, aux_local - tail)],
        [(last, aux_local - tail, tail)],
    ]
    arrivals = []
    for group in groups:
        piece = jnp.concatenate(
            [right_factor[:, t, start:start + count] for t, start, count in group], axis=1
        )
        piece = piece.at[kb_table].get(mode="promise_in_bounds")
        if arrivals:
            piece, arrivals[-1], bq, blocks, orbital = lax.optimization_barrier(
                (piece, arrivals[-1], bq, blocks, orbital)
            )
        arrivals.append(
            lax.all_to_all(piece, "ka", split_axis=0, concat_axis=2, tiled=True)[0]
        )
    ladder_t = jnp.zeros((pair_count * virtuals, virtuals), jnp.float32)
    tts = [trial_transposed(b, virtuals, pair_count) for b in blocks]
    for group, arrived in zip(groups, arrivals):
        slabs = sum(count for _, _, count in group)
        right = arrived.reshape(slabs, virtuals, virtuals)
        ct = jnp.swapaxes(right, 1, 2).reshape(slabs * virtuals, virtuals)
        at = 0
        for t, start, count in group:
            ladder_t = ladder_transposed(
                ct[at * virtuals:(at + count) * virtuals], tts[t],
                bq[t, start // 2:(start + count) // 2], ladder_t,
            )
            at += count
    ladder_sum = ladder_t.T
    cores = lax.axis_size("core")
    stacked = ladder_sum.reshape(vert // cores, cores, slab_width, -1)
    stacked = lax.all_to_all(stacked, "core", 1, 1, tiled=True).sum(1)
    ladder = lax.all_to_all(stacked, "zl", 0, 0, tiled=True).sum(0)
    combined = ladder + orbital
    return combined.astype(jnp.bfloat16)[None]


def solution(mesh):
    kpoints, vert = mesh.devices.shape
    cores = 2
    split = jax.sharding.Mesh(
        mesh.devices.reshape(kpoints, vert // cores, cores), ("ka", "zl", "core")
    )
    slab = ("zl", "core")
    in_specs = (
        P("ka", None, None),
        P("ka", None, slab, None),
        P(None, None, slab, "ka"),
        P(),
        P(),
        P(),
    )
    out_specs = P("ka", slab, None)
    return jax.shard_map(shards, mesh=split, in_specs=in_specs, out_specs=out_specs, check_vma=False)
```

```python
import functools

import jax
import jax.numpy as jnp
from jax import lax
from jax.experimental import pallas as pl
from jax.experimental.pallas import tpu as pltpu
from jax.sharding import PartitionSpec as P


def shifted(value, axis, steps):
    count = lax.axis_size(axis)
    pairs = [(source, (source + steps) % count) for source in range(count)]
    return lax.ppermute(value, axis, pairs)


def ladder_kernel(ct_ref, tt_ref, b_ref, acc_ref, out_ref, *, chunk, nv, pairs, lanes):
    j = pl.program_id(0)

    @pl.when(j == 0)
    def _():
        out_ref[...] = acc_ref[...]

    half = jnp.dot(ct_ref[...], tt_ref[...], preferred_element_type=jnp.float32)
    half = half.astype(jnp.bfloat16)
    acc = out_ref[...]
    for two in range(chunk // 2):
        stacked = []
        for l in (2 * two, 2 * two + 1):
            rows = half[l * nv:(l + 1) * nv]
            stacked.append(jnp.concatenate(
                [rows[:, p * lanes:(p + 1) * lanes] for p in range(pairs)], axis=0
            ))
        acc = acc + lax.dot_general(
            jnp.concatenate(stacked, axis=1), b_ref[two], (((1,), (1,)), ((), ())),
            preferred_element_type=jnp.float32,
        )
    out_ref[...] = acc


def ladder_transposed(ct, tt, bpair, acc, chunk=16):
    rows, nv = ct.shape
    aux = 2 * bpair.shape[0]
    lanes = 128
    pairs = tt.shape[1] // lanes
    steps = aux // chunk
    kernel = functools.partial(ladder_kernel, chunk=chunk, nv=nv, pairs=pairs, lanes=lanes)
    flops = 2 * aux * nv * nv * (pairs * lanes + pairs * nv)
    return pl.pallas_call(
        kernel,
        out_shape=jax.ShapeDtypeStruct((pairs * nv, nv), jnp.float32),
        grid=(steps,),
        in_specs=[
            pl.BlockSpec((chunk * nv, nv), lambda j: (j, 0)),
            pl.BlockSpec((nv, pairs * lanes), lambda j: (0, 0)),
            pl.BlockSpec((chunk // 2, nv, 2 * lanes), lambda j: (j, 0, 0)),
            pl.BlockSpec((pairs * nv, nv), lambda j: (0, 0)),
        ],
        out_specs=pl.BlockSpec((pairs * nv, nv), lambda j: (0, 0)),
        input_output_aliases={3: 0},
        compiler_params=pltpu.CompilerParams(
            dimension_semantics=("arbitrary",),
            vmem_limit_bytes=48 * 1024 * 1024,
        ),
        cost_estimate=pl.CostEstimate(
            flops=flops, transcendentals=0,
            bytes_accessed=2 * (ct.size + tt.size + bpair.size) + 8 * pairs * nv * nv,
        ),
    )(ct, tt, bpair, acc)


def left_pairs(left, virtuals):
    transfers, aux = left.shape[0], left.shape[1]
    b = left.reshape(transfers, aux // 2, 2, virtuals, virtuals)
    b = jnp.pad(b, ((0, 0), (0, 0), (0, 0), (0, 0), (0, 128 - virtuals)))
    b = jnp.transpose(b, (0, 1, 3, 2, 4))
    return b.reshape(transfers, aux // 2, virtuals, 256)


def trial_transposed(block, virtuals, pair_count):
    t = block.reshape(virtuals, pair_count, virtuals)
    t = jnp.transpose(t, (2, 1, 0))
    t = jnp.pad(t, ((0, 0), (0, 0), (0, 128 - virtuals)))
    return t.reshape(virtuals, pair_count * 128)


def shards(trial_vector, left_factor, right_factor, kb_table, vir_energy, pair_energy):
    kpoints = vir_energy.shape[0]
    virtuals = vir_energy.shape[1]
    transfers = left_factor.shape[1]
    aux_local = left_factor.shape[2]
    pair_count = trial_vector.shape[2] // virtuals
    own_block = trial_vector[0]
    vert = lax.axis_size(("zl", "core"))
    slab_width = virtuals // vert
    offset = lax.axis_index(("zl", "core")) * slab_width
    labels = jnp.arange(kpoints, dtype=jnp.int32)
    owner_index = lax.axis_index("ka")
    momentum_b = jnp.sum(jnp.where(labels == owner_index, kb_table, 0))
    energy_rows = jnp.sum(jnp.where((labels == owner_index)[:, None], vir_energy, 0.0), axis=0)
    energy_other = jnp.sum(jnp.where((labels == momentum_b)[:, None], vir_energy, 0.0), axis=0)
    energy_a = lax.dynamic_slice_in_dim(energy_rows, offset, slab_width, 0)
    own_rows = lax.dynamic_slice_in_dim(own_block, offset, slab_width, 0).astype(jnp.float32)
    own_rows = own_rows.reshape(slab_width, pair_count, virtuals)
    shift_energy = (
        energy_a[:, None, None] + energy_other[None, None, :] - pair_energy[None, :, None]
    )
    orbital = (shift_energy * own_rows).reshape(slab_width, pair_count * virtuals)
    bq = left_pairs(left_factor[0], virtuals)
    blocks = [own_block] + [
        shifted(trial_vector, "ka", transfer)[0] for transfer in range(1, transfers)
    ]
    tail = aux_local // 2
    last = transfers - 1
    groups = [
        [(t, 0, aux_local) for t in range(last)] + [(last, 0, aux_local - tail)],
        [(last, aux_local - tail, tail)],
    ]
    arrivals = []
    for group in groups:
        piece = jnp.concatenate(
            [right_factor[:, t, start:start + count] for t, start, count in group], axis=1
        )
        piece = piece.at[kb_table].get(mode="promise_in_bounds")
        if arrivals:
            piece, arrivals[-1], bq, blocks, orbital = lax.optimization_barrier(
                (piece, arrivals[-1], bq, blocks, orbital)
            )
        arrivals.append(
            lax.all_to_all(piece, "ka", split_axis=0, concat_axis=2, tiled=True)[0]
        )
    ladder_t = jnp.zeros((pair_count * virtuals, virtuals), jnp.float32)
    tts = [trial_transposed(b, virtuals, pair_count) for b in blocks]
    for group, arrived in zip(groups, arrivals):
        slabs = sum(count for _, _, count in group)
        right = arrived.reshape(slabs, virtuals, virtuals)
        ct = jnp.swapaxes(right, 1, 2).reshape(slabs * virtuals, virtuals)
        at = 0
        for t, start, count in group:
            ladder_t = ladder_transposed(
                ct[at * virtuals:(at + count) * virtuals], tts[t],
                bq[t, start // 2:(start + count) // 2], ladder_t,
            )
            at += count
    ladder_sum = ladder_t.T
    cores = lax.axis_size("core")
    stacked = ladder_sum.reshape(vert // cores, cores, slab_width, -1)
    stacked = lax.all_to_all(stacked, "core", 1, 1, tiled=True).sum(1)
    ladder = lax.all_to_all(stacked, "zl", 0, 0, tiled=True).sum(0)
    combined = ladder + orbital
    return combined.astype(jnp.bfloat16)[None]


def solution(mesh):
    kpoints, vert = mesh.devices.shape
    cores = 2
    split = jax.sharding.Mesh(
        mesh.devices.reshape(kpoints, vert // cores, cores), ("ka", "zl", "core")
    )
    slab = ("zl", "core")
    in_specs = (
        P("ka", None, None),
        P("ka", None, slab, None),
        P(None, None, slab, "ka"),
        P(),
        P(),
        P(),
    )
    out_specs = P("ka", slab, None)
    return jax.shard_map(shards, mesh=split, in_specs=in_specs, out_specs=out_specs, check_vma=False)
```

```python
import functools

import jax
import jax.numpy as jnp
from jax import lax
from jax.experimental import pallas as pl
from jax.experimental.pallas import tpu as pltpu
from jax.sharding import PartitionSpec as P


def shifted(value, axis, steps):
    count = lax.axis_size(axis)
    pairs = [(source, (source + steps) % count) for source in range(count)]
    return lax.ppermute(value, axis, pairs)


def ladder_kernel(ct_ref, tt_ref, b_ref, acc_ref, out_ref, *, chunk, nv, pairs, lanes):
    j = pl.program_id(0)

    @pl.when(j == 0)
    def _():
        out_ref[...] = acc_ref[...]

    half = jnp.dot(ct_ref[...], tt_ref[...], preferred_element_type=jnp.float32)
    half = half.astype(jnp.bfloat16)
    acc = out_ref[...]
    for two in range(chunk // 2):
        stacked = []
        for l in (2 * two, 2 * two + 1):
            rows = half[l * nv:(l + 1) * nv]
            stacked.append(jnp.concatenate(
                [rows[:, p * lanes:(p + 1) * lanes] for p in range(pairs)], axis=0
            ))
        acc = acc + lax.dot_general(
            jnp.concatenate(stacked, axis=1), b_ref[two], (((1,), (1,)), ((), ())),
            preferred_element_type=jnp.float32,
        )
    out_ref[...] = acc


def ladder_transposed(ct, tt, bpair, acc, chunk=4):
    rows, nv = ct.shape
    aux = 2 * bpair.shape[0]
    lanes = 128
    pairs = tt.shape[1] // lanes
    steps = aux // chunk
    kernel = functools.partial(ladder_kernel, chunk=chunk, nv=nv, pairs=pairs, lanes=lanes)
    flops = 2 * aux * nv * nv * (pairs * lanes + pairs * nv)
    return pl.pallas_call(
        kernel,
        out_shape=jax.ShapeDtypeStruct((pairs * nv, nv), jnp.float32),
        grid=(steps,),
        in_specs=[
            pl.BlockSpec((chunk * nv, nv), lambda j: (j, 0)),
            pl.BlockSpec((nv, pairs * lanes), lambda j: (0, 0)),
            pl.BlockSpec((chunk // 2, nv, 2 * lanes), lambda j: (j, 0, 0)),
            pl.BlockSpec((pairs * nv, nv), lambda j: (0, 0)),
        ],
        out_specs=pl.BlockSpec((pairs * nv, nv), lambda j: (0, 0)),
        input_output_aliases={3: 0},
        compiler_params=pltpu.CompilerParams(
            dimension_semantics=("arbitrary",),
            vmem_limit_bytes=48 * 1024 * 1024,
        ),
        cost_estimate=pl.CostEstimate(
            flops=flops, transcendentals=0,
            bytes_accessed=2 * (ct.size + tt.size + bpair.size) + 8 * pairs * nv * nv,
        ),
    )(ct, tt, bpair, acc)


def left_pairs(left, virtuals):
    transfers, aux = left.shape[0], left.shape[1]
    b = left.reshape(transfers, aux // 2, 2, virtuals, virtuals)
    b = jnp.pad(b, ((0, 0), (0, 0), (0, 0), (0, 0), (0, 128 - virtuals)))
    b = jnp.transpose(b, (0, 1, 3, 2, 4))
    return b.reshape(transfers, aux // 2, virtuals, 256)


def trial_transposed(block, virtuals, pair_count):
    t = block.reshape(virtuals, pair_count, virtuals)
    t = jnp.transpose(t, (2, 1, 0))
    t = jnp.pad(t, ((0, 0), (0, 0), (0, 128 - virtuals)))
    return t.reshape(virtuals, pair_count * 128)


def shards(trial_vector, left_factor, right_factor, kb_table, vir_energy, pair_energy):
    kpoints = vir_energy.shape[0]
    virtuals = vir_energy.shape[1]
    transfers = left_factor.shape[1]
    aux_local = left_factor.shape[2]
    pair_count = trial_vector.shape[2] // virtuals
    own_block = trial_vector[0]
    vert = lax.axis_size(("zl", "core"))
    slab_width = virtuals // vert
    offset = lax.axis_index(("zl", "core")) * slab_width
    labels = jnp.arange(kpoints, dtype=jnp.int32)
    owner_index = lax.axis_index("ka")
    momentum_b = jnp.sum(jnp.where(labels == owner_index, kb_table, 0))
    energy_rows = jnp.sum(jnp.where((labels == owner_index)[:, None], vir_energy, 0.0), axis=0)
    energy_other = jnp.sum(jnp.where((labels == momentum_b)[:, None], vir_energy, 0.0), axis=0)
    energy_a = lax.dynamic_slice_in_dim(energy_rows, offset, slab_width, 0)
    own_rows = lax.dynamic_slice_in_dim(own_block, offset, slab_width, 0).astype(jnp.float32)
    own_rows = own_rows.reshape(slab_width, pair_count, virtuals)
    shift_energy = (
        energy_a[:, None, None] + energy_other[None, None, :] - pair_energy[None, :, None]
    )
    orbital = (shift_energy * own_rows).reshape(slab_width, pair_count * virtuals)
    bq = left_pairs(left_factor[0], virtuals)
    blocks = [own_block] + [
        shifted(trial_vector, "ka", transfer)[0] for transfer in range(1, transfers)
    ]
    tail = aux_local // 2
    last = transfers - 1
    groups = [
        [(t, 0, aux_local) for t in range(last)] + [(last, 0, aux_local - tail)],
        [(last, aux_local - tail, tail)],
    ]
    arrivals = []
    for group in groups:
        piece = jnp.concatenate(
            [right_factor[:, t, start:start + count] for t, start, count in group], axis=1
        )
        piece = piece.at[kb_table].get(mode="promise_in_bounds")
        if arrivals:
            piece, arrivals[-1], bq, blocks, orbital = lax.optimization_barrier(
                (piece, arrivals[-1], bq, blocks, orbital)
            )
        arrivals.append(
            lax.all_to_all(piece, "ka", split_axis=0, concat_axis=2, tiled=True)[0]
        )
    ladder_t = jnp.zeros((pair_count * virtuals, virtuals), jnp.float32)
    tts = [trial_transposed(b, virtuals, pair_count) for b in blocks]
    for group, arrived in zip(groups, arrivals):
        slabs = sum(count for _, _, count in group)
        right = arrived.reshape(slabs, virtuals, virtuals)
        ct = jnp.swapaxes(right, 1, 2).reshape(slabs * virtuals, virtuals)
        at = 0
        for t, start, count in group:
            ladder_t = ladder_transposed(
                ct[at * virtuals:(at + count) * virtuals], tts[t],
                bq[t, start // 2:(start + count) // 2], ladder_t,
            )
            at += count
    ladder_sum = ladder_t.T
    cores = lax.axis_size("core")
    stacked = ladder_sum.reshape(vert // cores, cores, slab_width, -1)
    stacked = lax.all_to_all(stacked, "core", 1, 1, tiled=True).sum(1)
    ladder = lax.all_to_all(stacked, "zl", 0, 0, tiled=True).sum(0)
    combined = ladder + orbital
    return combined.astype(jnp.bfloat16)[None]


def solution(mesh):
    kpoints, vert = mesh.devices.shape
    cores = 2
    split = jax.sharding.Mesh(
        mesh.devices.reshape(kpoints, vert // cores, cores), ("ka", "zl", "core")
    )
    slab = ("zl", "core")
    in_specs = (
        P("ka", None, None),
        P("ka", None, slab, None),
        P(None, None, slab, "ka"),
        P(),
        P(),
        P(),
    )
    out_specs = P("ka", slab, None)
    return jax.shard_map(shards, mesh=split, in_specs=in_specs, out_specs=out_specs, check_vma=False)
```
